512 devices in a mesh: blk: 64 (over y_lo, z, core), exp: 8 (over y_hi, x).
Axes of the slice: x: 4, y: 4 (y_hi: 2, y_lo: 2; y = y_hi * 2 + y_lo), z: 16, core: 2. Of those that a mesh axis runs over, the one named last changes fastest.
Arguments:
- hidden_in: bfloat16 [32, 4, 2048], P('exp'), may hold values from -3 to 3
- q_lat: bfloat16 [32, 4, 16, 512], P('exp'), may hold values from -28 to 28
- q_rope: bfloat16 [32, 4, 16, 64], P('exp'), may hold values from -4 to 4
- new_lat: bfloat16 [32, 4, 512], P('exp'), may hold values from -4 to 4
- new_rope: bfloat16 [32, 4, 64], P('exp'), may hold values from -4 to 4
- cache_lat: bfloat16 [32, 16384, 512], P('exp', 'blk'), may hold values from -4 to 4
- cache_rope: bfloat16 [32, 16384, 64], P('exp', 'blk'), may hold values from -4 to 4
- lengths: int32 [32], P('exp'), may hold values from 2 to 16384, as said below
- w_uv: bfloat16 [512, 2048], P(None, 'blk'), may hold values from -3 to 3
- w_out: bfloat16 [2048, 2048], P('blk'), may hold values from -0.125 to 0.125
- norm_gain: float32 [2048], replicated, may hold values from 0.1 to 1.9
- w_router: bfloat16 [2048, 64], replicated, may hold values from -0.125 to 0.125
- routes: int32 [32, 4, 6], P('exp'), may hold values from 0 to 63, all different within a row; in each aligned block of 16 rows (0 to 15, 16 to 31, ..., all dimensions but the last counted through in order) at most 3 rows name the same one
- w_gate: bfloat16 [64, 2048, 1408], P('blk', None, 'exp'), may hold values from -0.125 to 0.125
- w_up: bfloat16 [64, 2048, 1408], P('blk', None, 'exp'), may hold values from -0.125 to 0.125
- w_down: bfloat16 [64, 1408, 2048], P('blk', 'exp'), may hold values from -0.15625 to 0.15625
Outputs:
- hidden_out: bfloat16 [32, 4, 2048], P('exp')
The draws below stay inside these ranges and needn't reach their ends.
Inputs may be any that keep to these rules, and one draw needn't show every extreme that they name: `lengths`: in each aligned group of 4 requests exactly 1 have length 16384; the others have 2 to 512. `routes`: each row names 6 different experts; in the 16 rows of one index of exp no expert is named more than 3 times.
All inputs are finite; a program needn't handle non-finite values.
Results may differ from the reference program's by a relative error of at most 0.0062.
Values may be sent and summed in bfloat16 or wider, within the bound.
No kernel may reach another device: no remote copies, remote signals or barrier semaphores. Data moves between devices by JAX's collectives and lax.ppermute only.
A program may use at most 128 MiB of HBM per device.

```python
import math
import jax
import jax.numpy as jnp
import numpy as np
from jax import lax

D = 2048
H = 16
C = 512
R = 64
V = 128
QK = 192
FE = 1408
EXPERTS = 64
TOP = 6
STEPS = 4
SHORT = 512
CAP = 3
REQ_DEV = 4
CB = 256
REQS = 32
LMAX = 16384


def draw_cache_lat(key, part):
    base = jnp.clip(jax.random.normal(jax.random.fold_in(key, 11), (REQS, LMAX, C), jnp.float32), -4.0, 4.0)
    return base.astype(jnp.bfloat16)


def draw_q_lat(key, part):
    base = jnp.clip(jax.random.normal(jax.random.fold_in(key, 21), (REQS, STEPS, H, C), jnp.float32), -4.0, 4.0)
    return base.astype(jnp.bfloat16)


def draw_lengths(key, part):
    groups = REQS // REQ_DEV
    group_keys = jax.random.split(jax.random.fold_in(key, 31), groups)
    orders = jax.vmap(lambda single: jax.random.permutation(single, REQ_DEV))(group_keys)
    short_lengths = jax.random.randint(jax.random.fold_in(key, 32), (groups, REQ_DEV), 2, SHORT + 1)
    long_mask = orders < REQ_DEV // 4
    return jnp.where(long_mask, LMAX, short_lengths).reshape(REQS).astype(jnp.int32)


def steps_of(own_key, extent, shards, smallest, largest):
    def one(position, shards_of):
        steps = jax.random.uniform(jax.random.fold_in(jax.random.fold_in(own_key, 6), position), (shards_of,), jnp.float32, smallest / len(shards), largest / len(shards))
        return jnp.repeat(jnp.exp(steps), extent[position] // shards_of).reshape((-1,) + (1,) * (len(extent) - position - 1))

    loudness = one(*shards[0])
    for cut in shards[1:]:
        loudness = loudness * one(*cut)
    return loudness


def deal_out(rng, own, number, rows, count, top, most, lean):
    ranking = jax.random.permutation(rng, count)
    heavy_load, ordinary = shares(count, rows * top, most, lean, True), shares(count, rows * top, most, lean, False)
    places = jnp.arange(count)

    def named(sizes, rotation):
        used = int((sizes > 0).sum())
        fixed = max(1, used // 4)
        shifted = fixed + (places - fixed + rotation * (used - fixed)) % max(1, count - fixed)
        return jnp.zeros((count,), jnp.int32).at[ranking[jnp.where(places < fixed, places, shifted)]].set(jnp.asarray(sizes, jnp.int32))

    sizes = jnp.where(number % 4 == 0, named(heavy_load, number // 4), named(ordinary, number - number // 4 - 1))
    mixed = jax.random.permutation(jax.random.fold_in(own, 3), count)
    source_of, receiver = mixed[0:count // 2 * 2:2], mixed[1:count // 2 * 2:2]
    slack = jnp.minimum(sizes[source_of] - 1, most - sizes[receiver]) // 2
    slack = jnp.where((source_of == ranking[0]) | (receiver == ranking[0]) | (sizes[receiver] == 0), 0, jnp.maximum(slack, 0))
    shifted = jax.random.randint(jax.random.fold_in(own, 4), (count // 2,), 0, 1 << 20) % (slack + 1)
    sizes = sizes.at[source_of].add(-shifted).at[receiver].add(shifted)
    members = jnp.searchsorted(jnp.cumsum(sizes), jnp.arange(rows * top), side="right").astype(jnp.int32)
    listing = members.reshape(top, rows).T
    listing = listing[jax.random.permutation(jax.random.fold_in(own, 1), rows)]
    rotation = jax.random.randint(jax.random.fold_in(own, 2), (rows, 1), 0, top)
    return jnp.take_along_axis(listing, (jnp.arange(top)[None, :] + rotation) % top, axis=1)


def shares(number_of, total, bound, lean, full):
    loads = [(1 << 20) // math.isqrt(grade ** lean) + 1 for grade in range(1, number_of + 1)]
    largest = bound if full else min(bound, max(-(-total // number_of), total * loads[0] // sum(loads)))
    least = 1 if total - largest >= number_of - 1 else 0
    given, rest = [largest] + [least] * (number_of - 1), total - largest - least * (number_of - 1)
    while rest > 0:
        candidates = [i for i in range(1, number_of) if given[i] < largest] or [i for i in range(1, number_of) if given[i] < bound]
        mass, remaining = sum([loads[i] for i in candidates]), rest
        for i in candidates:
            extra = min(bound - given[i], max(1, remaining * loads[i] // mass), rest)
            given[i] = given[i] + extra
            rest = rest - extra
    return np.array(given)


def scatter_about(key, shape, deviation, reach, shards=(), kind=jnp.bfloat16):
    loudness = steps_of(key, shape, shards, -0.22, 0.18) if shards else 1.0
    values = jax.random.normal(key, shape, jnp.float32) * deviation * loudness
    return jnp.minimum(jnp.maximum(values, -reach), reach).astype(kind)


def setup_inputs(seed: int = 0) -> dict:
    splits = jax.random.split(jax.random.key(seed), 17)
    hidden_in = scatter_about(splits[0], (REQS, STEPS, D), 0.5, 3.0, ((0, 8),))
    q_lat = draw_q_lat(jax.random.fold_in(splits[16], 71), 0)
    q_rope = scatter_about(splits[2], (REQS, STEPS, H, R), 1.0, 4.0, ((0, 8),))
    new_lat = scatter_about(splits[3], (REQS, STEPS, C), 1.0, 4.0, ((0, 8),))
    new_rope = scatter_about(splits[4], (REQS, STEPS, R), 1.0, 4.0, ((0, 8),))
    cache_lat = draw_cache_lat(jax.random.fold_in(splits[16], 71), 0)
    cache_rope = scatter_about(splits[6], (REQS, LMAX, R), 1.0, 4.0, ((0, 8), (1, 64)))
    lengths = draw_lengths(jax.random.fold_in(splits[16], 71), 0)
    w_uv = scatter_about(splits[8], (C, H * V), 0.5, 3.0, ((1, 64),))
    w_out = scatter_about(splits[9], (H * V, D), (H * V) ** -0.5, 0.125, ((0, 64),))
    norm_gain = jnp.clip(1.0 + 0.18 * jax.random.normal(splits[10], (D,), jnp.float32), 0.1, 1.9)
    w_router = scatter_about(splits[11], (D, EXPERTS), D ** -0.5, 0.125)
    routes_keys = jax.random.split(jax.random.fold_in(splits[12], 1), REQS * STEPS // (REQ_DEV * STEPS))
    routes_turns = jax.random.permutation(jax.random.fold_in(splits[12], 3), REQS * STEPS // (REQ_DEV * STEPS))
    routes = jax.vmap(lambda own, number: deal_out(jax.random.fold_in(splits[12], 2), own, number, REQ_DEV * STEPS, EXPERTS, TOP, CAP, 1))(routes_keys, routes_turns).reshape((REQS, STEPS, TOP))
    w_gate = scatter_about(splits[13], (EXPERTS, D, FE), D ** -0.5, 0.125, ((0, 64), (2, 8)))
    w_up = scatter_about(splits[14], (EXPERTS, D, FE), D ** -0.5, 0.125, ((0, 64), (2, 8)))
    w_down = scatter_about(splits[15], (EXPERTS, FE, D), FE ** -0.5, 0.15625, ((0, 64), (1, 8)))
    return dict(hidden_in=hidden_in, q_lat=q_lat, q_rope=q_rope, new_lat=new_lat, new_rope=new_rope, cache_lat=cache_lat, cache_rope=cache_rope, lengths=lengths, w_uv=w_uv, w_out=w_out, norm_gain=norm_gain, w_router=w_router, routes=routes, w_gate=w_gate, w_up=w_up, w_down=w_down)


NEG_FILL = -1e+30
ROUTE_SCALE = 2.446
NORM_EPS = 1e-06

def request_attention(args):
    query, query_rope, keys_lat, keys_rope, fresh_lat, fresh_rope, length = args
    scale = QK ** (-0.5)
    query_rows = query.reshape(STEPS * H, C).astype(jnp.float32)
    rope_rows = query_rope.reshape(STEPS * H, R).astype(jnp.float32)
    blocks = LMAX // CB
    key_blocks = keys_lat.astype(jnp.float32).reshape(blocks, CB, C)
    rope_blocks = keys_rope.astype(jnp.float32).reshape(blocks, CB, R)
    scores = (jnp.einsum('mc,bkc->mbk', query_rows, key_blocks) + jnp.einsum('mc,bkc->mbk', rope_rows, rope_blocks)) * scale
    valid = (jnp.arange(LMAX) < length).reshape(1, blocks, CB)
    masked = jnp.where(valid, scores, NEG_FILL)
    peaks = lax.optimization_barrier(jnp.max(masked, axis=2))
    weights = jnp.where(valid, jnp.exp(masked - peaks[:, :, None]), 0.0)
    totals = lax.optimization_barrier(jnp.sum(weights, axis=2))
    rounded = lax.optimization_barrier(weights.astype(jnp.bfloat16)).astype(jnp.float32)
    sums = jnp.einsum('mbk,bkc->mbc', rounded, key_blocks)
    fresh_scores = (jnp.dot(query_rows, fresh_lat.astype(jnp.float32).T) + jnp.dot(rope_rows, fresh_rope.astype(jnp.float32).T)) * scale
    token_of_row = jnp.arange(STEPS * H) // H
    fresh_valid = jnp.arange(STEPS)[None, :] <= token_of_row[:, None]
    fresh_masked = jnp.where(fresh_valid, fresh_scores, NEG_FILL)
    fresh_peak = lax.optimization_barrier(jnp.max(fresh_masked, axis=1))
    fresh_weights = jnp.where(fresh_valid, jnp.exp(fresh_masked - fresh_peak[:, None]), 0.0)
    fresh_total = lax.optimization_barrier(jnp.sum(fresh_weights, axis=1))
    fresh_rounded = lax.optimization_barrier(fresh_weights.astype(jnp.bfloat16)).astype(jnp.float32)
    fresh_sum = jnp.dot(fresh_rounded, fresh_lat.astype(jnp.float32), precision=lax.Precision.HIGHEST)
    peak_all = jnp.maximum(lax.optimization_barrier(jnp.max(peaks, axis=1)), fresh_peak)
    factors = jnp.exp(peaks - peak_all[:, None])
    fresh_factor = jnp.exp(fresh_peak - peak_all)
    grand_total = lax.optimization_barrier(jnp.sum(factors * totals, axis=1)) + fresh_factor * fresh_total
    grand_sum = jnp.einsum('mb,mbc->mc', factors, sums, precision=lax.Precision.HIGHEST) + fresh_factor[:, None] * fresh_sum
    return (grand_sum / grand_total[:, None]).astype(jnp.bfloat16).reshape(STEPS, H, C)

def one_expert(args):
    expert_rows, gate_w, up_w, down_w = args
    gate = jnp.dot(expert_rows, gate_w, preferred_element_type=jnp.float32)
    upper = jnp.dot(expert_rows, up_w, preferred_element_type=jnp.float32)
    hidden = (jax.nn.silu(gate) * upper).astype(jnp.bfloat16)
    return jnp.dot(hidden, down_w, preferred_element_type=jnp.float32)

def reference(hidden_in, q_lat, q_rope, new_lat, new_rope, cache_lat, cache_rope, lengths, w_uv, w_out, norm_gain, w_router, routes, w_gate, w_up, w_down):
    lat_out = lax.map(request_attention, (q_lat, q_rope, cache_lat, cache_rope, new_lat, new_rope, lengths))
    token_rows = REQS * STEPS
    lat_rows = lat_out.reshape(token_rows, H, C).astype(jnp.float32)
    uv_heads = w_uv.astype(jnp.float32).reshape(C, H, V)
    heads_out = jnp.einsum('nhc,chv->nhv', lat_rows, uv_heads).astype(jnp.bfloat16).reshape(token_rows, H * V)
    mixed = hidden_in.reshape(token_rows, D).astype(jnp.float32) + jnp.dot(heads_out, w_out, preferred_element_type=jnp.float32)
    meansq = lax.optimization_barrier(jnp.mean(mixed * mixed, axis=1, keepdims=True))
    normed = (mixed * lax.rsqrt(meansq + NORM_EPS) * norm_gain[None, :]).astype(jnp.bfloat16)
    affinity = jax.nn.sigmoid(jnp.dot(normed, w_router, preferred_element_type=jnp.float32))
    flat_routes = routes.reshape(token_rows, TOP)
    chosen = jnp.take_along_axis(affinity, flat_routes, axis=1)
    route_weight = ROUTE_SCALE * chosen / lax.optimization_barrier(jnp.sum(chosen, axis=1, keepdims=True))
    groups = REQS // REQ_DEV
    group_rows = REQ_DEV * STEPS
    pair_routes = flat_routes.reshape(groups, group_rows * TOP)
    hits = (pair_routes[:, :, None] == jnp.arange(EXPERTS)[None, None, :]).astype(jnp.int32)
    ranks = jnp.cumsum(hits, axis=1) - 1
    slot_match = hits[:, :, :, None] * (ranks[:, :, :, None] == jnp.arange(CAP)[None, None, None, :]).astype(jnp.int32)
    select = slot_match.reshape(groups, group_rows, TOP, EXPERTS, CAP).astype(jnp.float32)
    dispatch_map = lax.optimization_barrier(jnp.sum(select, axis=2))
    combine_map = lax.optimization_barrier(jnp.sum(select * route_weight.reshape(groups, group_rows, TOP)[:, :, :, None, None], axis=2))
    normed_groups = normed.reshape(groups, group_rows, D).astype(jnp.float32)
    dispatched = jnp.einsum('grec,grd->egcd', dispatch_map, normed_groups).reshape(EXPERTS, groups * CAP, D).astype(jnp.bfloat16)
    outputs = lax.map(one_expert, (dispatched, w_gate, w_up, w_down))
    moe = jnp.einsum('grec,egcd->grd', combine_map, outputs.reshape(EXPERTS, groups, CAP, D), precision=lax.Precision.HIGHEST)
    result = mixed + moe.reshape(token_rows, D)
    return result.astype(jnp.bfloat16).reshape(REQS, STEPS, D)
```

```python
import jax
import jax.numpy as jnp
from jax import lax
from jax.sharding import PartitionSpec as P

V = 128
QK = 192
CAP = 3


NEG_FILL = -1e30
ROUTE_SCALE = 2.446
NORM_EPS = 1e-06


def xor_pairs(count, mask):
    return [(i, i ^ mask) for i in range(count)]


def exchange(x, axis, mask):
    count = lax.axis_size(axis)
    return jax.tree.map(lambda part: lax.ppermute(part, axis, xor_pairs(count, mask)), x)


def exchange_state(state, axis, mask):
    peak_val, weight_sum, summed = state
    packed = jnp.concatenate([summed, peak_val[..., None], weight_sum[..., None]], axis=-1)
    got = exchange(packed, axis, mask)
    width = summed.shape[-1]
    return (got[..., width], got[..., width + 1], got[..., :width])


def butterfly_sum(x, axis, bits):
    for bit in bits:
        x = x + exchange(x, axis, 1 << bit)
    return x


def butterfly_gather(x, axis, bits):
    me = lax.axis_index(axis)
    x = x[None]
    for bit in bits:
        other = exchange(x, axis, 1 << bit)
        high = ((me >> bit) & 1) == 1
        low_part = jnp.where(high, other, x)
        high_part = jnp.where(high, x, other)
        x = jnp.concatenate([low_part, high_part], axis=0)
    return x


def butterfly_scatter_sum(x, axis, bits):
    me = lax.axis_index(axis)
    for bit in bits:
        side = (me >> bit) & 1
        keep = lax.dynamic_index_in_dim(x, side, 0, keepdims=False)
        send = lax.dynamic_index_in_dim(x, 1 - side, 0, keepdims=False)
        x = keep + exchange(send, axis, 1 << bit)
    return x


def block_partial(query, query_rope, keys_lat, keys_rope, valid):
    scale = QK ** (-0.5)
    scores = (
        jnp.einsum("rmc,rkc->rmk", query, keys_lat, preferred_element_type=jnp.float32)
        + jnp.einsum("rmc,rkc->rmk", query_rope, keys_rope, preferred_element_type=jnp.float32)
    ) * scale
    masked = jnp.where(valid, scores, NEG_FILL)
    peak_val = jnp.max(masked, axis=2)
    weights = jnp.where(valid, jnp.exp(masked - peak_val[:, :, None]), 0.0)
    weight_sum = jnp.sum(weights, axis=2)
    summed = jnp.einsum(
        "rmk,rkc->rmc", weights.astype(jnp.bfloat16), keys_lat, preferred_element_type=jnp.float32
    )
    return (peak_val, weight_sum, summed)


def merge_pair(left_part, right_part):
    peak_left, total_left, sum_left = left_part
    peak_right, total_right, sum_right = right_part
    peak_val = jnp.maximum(peak_left, peak_right)
    factor_left = jnp.exp(peak_left - peak_val)
    factor_right = jnp.exp(peak_right - peak_val)
    weight_sum = factor_left * total_left + factor_right * total_right
    summed = factor_left[..., None] * sum_left + factor_right[..., None] * sum_right
    return (peak_val, weight_sum, summed)


def local(
    hidden_in,
    q_lat,
    q_rope,
    new_lat,
    new_rope,
    cache_lat,
    cache_rope,
    lengths,
    w_uv,
    w_out,
    norm_gain,
    w_router,
    routes,
    w_gate,
    w_up,
    w_down,
):
    requests, new_steps, head_count, latent_dim = q_lat.shape
    me = lax.axis_index("blk")
    blk_bits = lax.axis_size("blk").bit_length() - 1
    exp_bits = lax.axis_size("exp").bit_length() - 1
    query_rows = new_steps * head_count
    query = q_lat.reshape(requests, query_rows, latent_dim)
    query_rope = q_rope.reshape(requests, query_rows, q_rope.shape[3])
    cache_span = cache_lat.shape[1]
    position = me * cache_span + lax.iota(jnp.int32, cache_span)
    cache_valid = jnp.broadcast_to(
        position[None, None, :] < lengths[:, None, None], (requests, query_rows, cache_span)
    )
    peak_val, weight_sum, summed = block_partial(query, query_rope, cache_lat, cache_rope, cache_valid)
    head_bits = head_count.bit_length() - 1
    split = (2,) * head_bits
    state = (
        peak_val.reshape(requests, new_steps, head_count).transpose(2, 0, 1).reshape(split + (requests, new_steps)),
        weight_sum.reshape(requests, new_steps, head_count).transpose(2, 0, 1).reshape(split + (requests, new_steps)),
        summed.reshape(requests, new_steps, head_count, latent_dim)
        .transpose(2, 0, 1, 3)
        .reshape(split + (requests, new_steps, latent_dim)),
    )
    low_bits = blk_bits - head_bits
    order = [head_bits - 1] + list(range(head_bits - 1))
    remaining = list(range(head_bits - 1, -1, -1))
    for head_bit in order:
        axis_pos = remaining.index(head_bit)
        remaining.pop(axis_pos)
        bit = head_bit + low_bits
        side = (me >> bit) & 1
        keep = jax.tree.map(lambda part: lax.dynamic_index_in_dim(part, side, axis_pos, keepdims=False), state)
        send = jax.tree.map(lambda part: lax.dynamic_index_in_dim(part, 1 - side, axis_pos, keepdims=False), state)
        state = merge_pair(keep, exchange_state(send, "blk", 1 << bit))
    for bit in range(low_bits - 1, -1, -1):
        state = merge_pair(state, exchange_state(state, "blk", 1 << bit))
    head_pick = me >> low_bits
    own_query = lax.dynamic_index_in_dim(q_lat, head_pick, axis=2, keepdims=False)
    own_rope = lax.dynamic_index_in_dim(q_rope, head_pick, axis=2, keepdims=False)
    fresh_valid = lax.iota(jnp.int32, new_steps)[None, :] <= lax.iota(jnp.int32, new_steps)[:, None]
    fresh_valid = jnp.broadcast_to(fresh_valid[None, :, :], (requests, new_steps, new_steps))
    fresh_part = block_partial(own_query, own_rope, new_lat, new_rope, fresh_valid)
    peak_val, weight_sum, summed = merge_pair(state, fresh_part)
    lat_out = (summed / weight_sum[:, :, None]).astype(jnp.bfloat16)
    token_rows = requests * new_steps
    lat_head = lat_out.reshape(token_rows, latent_dim)
    heads_out = jnp.dot(lat_head, w_uv, preferred_element_type=jnp.float32).astype(jnp.bfloat16)
    proj_part = jnp.dot(heads_out, w_out, preferred_element_type=jnp.float32)
    projected = butterfly_sum(proj_part, "blk", range(blk_bits))
    width = hidden_in.shape[2]
    mixed = hidden_in.reshape(token_rows, width).astype(jnp.float32) + projected
    meansq = jnp.mean(mixed * mixed, axis=1, keepdims=True)
    normed = (mixed * lax.rsqrt(meansq + NORM_EPS) * norm_gain[None, :]).astype(jnp.bfloat16)
    affinity = jax.nn.sigmoid(jnp.dot(normed, w_router, preferred_element_type=jnp.float32))
    expert_total = w_router.shape[1]
    top_count = routes.shape[2]
    flat_routes = routes.reshape(token_rows, top_count)
    route_hits = flat_routes[:, :, None] == lax.iota(jnp.int32, expert_total)[None, None, :]
    chosen = jnp.sum(jnp.where(route_hits, affinity[:, None, :], 0.0), axis=2)
    route_weight = ROUTE_SCALE * chosen / jnp.sum(chosen, axis=1, keepdims=True)
    local_count = w_gate.shape[0]
    local_ids = me * local_count + lax.iota(jnp.int32, local_count)
    pair_routes = flat_routes.reshape(token_rows * top_count)
    local_hits = (pair_routes[:, None] == local_ids[None, :]).astype(jnp.int32)
    ranks = jnp.cumsum(local_hits, axis=0) - 1
    slot_ids = lax.iota(jnp.int32, CAP)
    slot_match = local_hits.T[:, None, :] * (ranks.T[:, None, :] == slot_ids[None, :, None]).astype(
        jnp.int32
    )
    select = slot_match.reshape(local_count, CAP, token_rows, top_count).astype(jnp.float32)
    dispatch_map = jnp.sum(select, axis=3)
    combine_map = jnp.sum(select * route_weight[None, None, :, :], axis=3)
    dispatched = jnp.einsum(
        "esr,rd->esd", dispatch_map.astype(jnp.bfloat16), normed, preferred_element_type=jnp.float32
    ).astype(jnp.bfloat16)
    gathered = butterfly_gather(dispatched, "exp", range(exp_bits))
    groups = gathered.shape[0]
    piece = gathered.transpose(1, 0, 2, 3).reshape(local_count, groups * CAP, width)
    gate = jnp.einsum("erd,edf->erf", piece, w_gate, preferred_element_type=jnp.float32)
    upper = jnp.einsum("erd,edf->erf", piece, w_up, preferred_element_type=jnp.float32)
    hidden_all = (jax.nn.silu(gate) * upper).astype(jnp.bfloat16)
    partial_out = jnp.einsum("erf,efd->erd", hidden_all, w_down, preferred_element_type=jnp.float32)
    split_out = partial_out.reshape((local_count,) + (2,) * exp_bits + (CAP, width))
    split_out = jnp.moveaxis(split_out, 0, exp_bits)
    expert_out = butterfly_scatter_sum(split_out, "exp", range(exp_bits - 1, -1, -1))
    moe_part = jnp.einsum("esr,esd->rd", combine_map, expert_out, precision=lax.Precision.HIGHEST)
    moe_all = butterfly_sum(moe_part, "blk", range(blk_bits))
    result = (mixed + moe_all).astype(jnp.bfloat16)
    return result.reshape(requests, new_steps, width)


def solution(mesh):
    in_specs = (
        P("exp", None, None),
        P("exp", None, None, None),
        P("exp", None, None, None),
        P("exp", None, None),
        P("exp", None, None),
        P("exp", "blk", None),
        P("exp", "blk", None),
        P("exp"),
        P(None, "blk"),
        P("blk", None),
        P(),
        P(),
        P("exp", None, None),
        P("blk", None, "exp"),
        P("blk", None, "exp"),
        P("blk", "exp", None),
    )
    out_specs = P("exp", None, None)
    return jax.shard_map(local, mesh=mesh, in_specs=in_specs, out_specs=out_specs, check_vma=False)
```

```python
import jax
import jax.numpy as jnp
from jax import lax
from jax.sharding import PartitionSpec as P

V = 128
QK = 192
CAP = 3


NEG_FILL = -1e30
ROUTE_SCALE = 2.446
NORM_EPS = 1e-06


def xor_pairs(count, mask):
    return [(i, i ^ mask) for i in range(count)]


def exchange(x, axis, mask):
    count = lax.axis_size(axis)
    return jax.tree.map(lambda part: lax.ppermute(part, axis, xor_pairs(count, mask)), x)


def exchange_state(state, axis, mask):
    peak_val, weight_sum, summed = state
    packed = jnp.concatenate([summed, peak_val[..., None], weight_sum[..., None]], axis=-1)
    got = exchange(packed, axis, mask)
    width = summed.shape[-1]
    return (got[..., width], got[..., width + 1], got[..., :width])


def butterfly_sum(x, axis, bits):
    for bit in bits:
        x = x + exchange(x, axis, 1 << bit)
    return x


def butterfly_gather(x, axis, bits):
    me = lax.axis_index(axis)
    x = x[None]
    for bit in bits:
        other = exchange(x, axis, 1 << bit)
        high = ((me >> bit) & 1) == 1
        low_part = jnp.where(high, other, x)
        high_part = jnp.where(high, x, other)
        x = jnp.concatenate([low_part, high_part], axis=0)
    return x


def butterfly_scatter_sum(x, axis, bits):
    me = lax.axis_index(axis)
    for bit in bits:
        side = (me >> bit) & 1
        keep = lax.dynamic_index_in_dim(x, side, 0, keepdims=False)
        send = lax.dynamic_index_in_dim(x, 1 - side, 0, keepdims=False)
        x = keep + exchange(send, axis, 1 << bit)
    return x


def block_partial(query, query_rope, keys_lat, keys_rope, valid):
    scale = QK ** (-0.5)
    scores = (
        jnp.einsum("rmc,rkc->rmk", query, keys_lat, preferred_element_type=jnp.float32)
        + jnp.einsum("rmc,rkc->rmk", query_rope, keys_rope, preferred_element_type=jnp.float32)
    ) * scale
    masked = jnp.where(valid, scores, NEG_FILL)
    peak_val = jnp.max(masked, axis=2)
    weights = jnp.where(valid, jnp.exp(masked - peak_val[:, :, None]), 0.0)
    weight_sum = jnp.sum(weights, axis=2)
    summed = jnp.einsum(
        "rmk,rkc->rmc", weights.astype(jnp.bfloat16), keys_lat, preferred_element_type=jnp.float32
    )
    return (peak_val, weight_sum, summed)


def merge_pair(left_part, right_part):
    peak_left, total_left, sum_left = left_part
    peak_right, total_right, sum_right = right_part
    peak_val = jnp.maximum(peak_left, peak_right)
    factor_left = jnp.exp(peak_left - peak_val)
    factor_right = jnp.exp(peak_right - peak_val)
    weight_sum = factor_left * total_left + factor_right * total_right
    summed = factor_left[..., None] * sum_left + factor_right[..., None] * sum_right
    return (peak_val, weight_sum, summed)


def local(
    hidden_in,
    q_lat,
    q_rope,
    new_lat,
    new_rope,
    cache_lat,
    cache_rope,
    lengths,
    w_uv,
    w_out,
    norm_gain,
    w_router,
    routes,
    w_gate,
    w_up,
    w_down,
):
    requests, new_steps, head_count, latent_dim = q_lat.shape
    me = lax.axis_index("blk")
    blk_bits = lax.axis_size("blk").bit_length() - 1
    exp_bits = lax.axis_size("exp").bit_length() - 1
    query_rows = new_steps * head_count
    query = q_lat.reshape(requests, query_rows, latent_dim)
    query_rope = q_rope.reshape(requests, query_rows, q_rope.shape[3])
    cache_span = cache_lat.shape[1]
    position = me * cache_span + lax.iota(jnp.int32, cache_span)
    cache_valid = jnp.broadcast_to(
        position[None, None, :] < lengths[:, None, None], (requests, query_rows, cache_span)
    )
    peak_val, weight_sum, summed = block_partial(query, query_rope, cache_lat, cache_rope, cache_valid)
    head_bits = head_count.bit_length() - 1
    split = (2,) * head_bits
    state = (
        peak_val.reshape(requests, new_steps, head_count).transpose(2, 0, 1).reshape(split + (requests, new_steps)),
        weight_sum.reshape(requests, new_steps, head_count).transpose(2, 0, 1).reshape(split + (requests, new_steps)),
        summed.reshape(requests, new_steps, head_count, latent_dim)
        .transpose(2, 0, 1, 3)
        .reshape(split + (requests, new_steps, latent_dim)),
    )
    low_bits = blk_bits - head_bits
    order = [head_bits - 1] + list(range(head_bits - 1))
    remaining = list(range(head_bits - 1, -1, -1))
    for head_bit in order:
        axis_pos = remaining.index(head_bit)
        remaining.pop(axis_pos)
        bit = head_bit + low_bits
        side = (me >> bit) & 1
        keep = jax.tree.map(lambda part: lax.dynamic_index_in_dim(part, side, axis_pos, keepdims=False), state)
        send = jax.tree.map(lambda part: lax.dynamic_index_in_dim(part, 1 - side, axis_pos, keepdims=False), state)
        state = merge_pair(keep, exchange_state(send, "blk", 1 << bit))
    for bit in range(low_bits - 1, -1, -1):
        state = merge_pair(state, exchange_state(state, "blk", 1 << bit))
    head_pick = me >> low_bits
    own_query = lax.dynamic_index_in_dim(q_lat, head_pick, axis=2, keepdims=False)
    own_rope = lax.dynamic_index_in_dim(q_rope, head_pick, axis=2, keepdims=False)
    fresh_valid = lax.iota(jnp.int32, new_steps)[None, :] <= lax.iota(jnp.int32, new_steps)[:, None]
    fresh_valid = jnp.broadcast_to(fresh_valid[None, :, :], (requests, new_steps, new_steps))
    fresh_part = block_partial(own_query, own_rope, new_lat, new_rope, fresh_valid)
    peak_val, weight_sum, summed = merge_pair(state, fresh_part)
    lat_out = (summed / weight_sum[:, :, None]).astype(jnp.bfloat16)
    token_rows = requests * new_steps
    lat_head = lat_out.reshape(token_rows, latent_dim)
    heads_out = jnp.dot(lat_head, w_uv, preferred_element_type=jnp.float32).astype(jnp.bfloat16)
    proj_part = jnp.dot(heads_out, w_out, preferred_element_type=jnp.float32)
    projected = butterfly_sum(proj_part, "blk", range(blk_bits))
    width = hidden_in.shape[2]
    mixed = hidden_in.reshape(token_rows, width).astype(jnp.float32) + projected
    meansq = jnp.mean(mixed * mixed, axis=1, keepdims=True)
    normed = (mixed * lax.rsqrt(meansq + NORM_EPS) * norm_gain[None, :]).astype(jnp.bfloat16)
    affinity = jax.nn.sigmoid(jnp.dot(normed, w_router, preferred_element_type=jnp.float32))
    expert_total = w_router.shape[1]
    top_count = routes.shape[2]
    flat_routes = routes.reshape(token_rows, top_count)
    route_hits = flat_routes[:, :, None] == lax.iota(jnp.int32, expert_total)[None, None, :]
    chosen = jnp.sum(jnp.where(route_hits, affinity[:, None, :], 0.0), axis=2)
    route_weight = ROUTE_SCALE * chosen / jnp.sum(chosen, axis=1, keepdims=True)
    local_count = w_gate.shape[0]
    local_ids = me * local_count + lax.iota(jnp.int32, local_count)
    pair_routes = flat_routes.reshape(token_rows * top_count)
    local_hits = (pair_routes[:, None] == local_ids[None, :]).astype(jnp.int32)
    ranks = jnp.cumsum(local_hits, axis=0) - 1
    slot_ids = lax.iota(jnp.int32, CAP)
    slot_match = local_hits.T[:, None, :] * (ranks.T[:, None, :] == slot_ids[None, :, None]).astype(
        jnp.int32
    )
    select = slot_match.reshape(local_count, CAP, token_rows, top_count).astype(jnp.float32)
    dispatch_map = jnp.sum(select, axis=3)
    combine_map = jnp.sum(select * route_weight[None, None, :, :], axis=3)
    dispatched = jnp.einsum(
        "esr,rd->esd", dispatch_map.astype(jnp.bfloat16), normed, preferred_element_type=jnp.float32
    ).astype(jnp.bfloat16)
    gate_w = lax.all_gather(w_gate, "exp", axis=2, tiled=True)
    up_w = lax.all_gather(w_up, "exp", axis=2, tiled=True)
    down_w = lax.all_gather(w_down, "exp", axis=1, tiled=True)
    gate = jnp.einsum("erd,edf->erf", dispatched, gate_w, preferred_element_type=jnp.float32)
    upper = jnp.einsum("erd,edf->erf", dispatched, up_w, preferred_element_type=jnp.float32)
    hidden_all = (jax.nn.silu(gate) * upper).astype(jnp.bfloat16)
    expert_out = jnp.einsum("erf,efd->erd", hidden_all, down_w, preferred_element_type=jnp.float32)
    moe_part = jnp.einsum("esr,esd->rd", combine_map, expert_out, precision=lax.Precision.HIGHEST)
    moe_all = butterfly_sum(moe_part, "blk", range(blk_bits))
    result = (mixed + moe_all).astype(jnp.bfloat16)
    return result.reshape(requests, new_steps, width)


def solution(mesh):
    in_specs = (
        P("exp", None, None),
        P("exp", None, None, None),
        P("exp", None, None, None),
        P("exp", None, None),
        P("exp", None, None),
        P("exp", "blk", None),
        P("exp", "blk", None),
        P("exp"),
        P(None, "blk"),
        P("blk", None),
        P(),
        P(),
        P("exp", None, None),
        P("blk", None, "exp"),
        P("blk", None, "exp"),
        P("blk", "exp", None),
    )
    out_specs = P("exp", None, None)
    return jax.shard_map(local, mesh=mesh, in_specs=in_specs, out_specs=out_specs, check_vma=False)
```

```python
import jax
import jax.numpy as jnp
from jax import lax
from jax.sharding import PartitionSpec as P

V = 128
QK = 192
CAP = 3


NEG_FILL = -1e30
ROUTE_SCALE = 2.446
NORM_EPS = 1e-06


def xor_pairs(count, mask):
    return [(i, i ^ mask) for i in range(count)]


def exchange(x, axis, mask):
    count = lax.axis_size(axis)
    return jax.tree.map(lambda part: lax.ppermute(part, axis, xor_pairs(count, mask)), x)


def exchange_state(state, axis, mask):
    peak_val, weight_sum, summed = state
    packed = jnp.concatenate([summed, peak_val[..., None], weight_sum[..., None]], axis=-1)
    got = exchange(packed, axis, mask)
    width = summed.shape[-1]
    return (got[..., width], got[..., width + 1], got[..., :width])


def butterfly_sum(x, axis, bits):
    for bit in bits:
        x = x + exchange(x, axis, 1 << bit)
    return x


def butterfly_gather(x, axis, bits):
    me = lax.axis_index(axis)
    x = x[None]
    for bit in bits:
        other = exchange(x, axis, 1 << bit)
        high = ((me >> bit) & 1) == 1
        low_part = jnp.where(high, other, x)
        high_part = jnp.where(high, x, other)
        x = jnp.concatenate([low_part, high_part], axis=0)
    return x


def butterfly_scatter_sum(x, axis, bits):
    me = lax.axis_index(axis)
    for bit in bits:
        side = (me >> bit) & 1
        keep = lax.dynamic_index_in_dim(x, side, 0, keepdims=False)
        send = lax.dynamic_index_in_dim(x, 1 - side, 0, keepdims=False)
        x = keep + exchange(send, axis, 1 << bit)
    return x


def a2a_sum(x, axis):
    count = lax.axis_size(axis)
    rows, cols = x.shape
    parts = x.reshape(rows, count, cols // count).transpose(1, 0, 2)
    mine = lax.all_to_all(parts, axis, 0, 0, tiled=True).sum(axis=0)
    spread = jnp.broadcast_to(mine[None], (count,) + mine.shape)
    back = lax.all_to_all(spread, axis, 0, 0, tiled=True)
    return back.transpose(1, 0, 2).reshape(rows, cols)


def a2a_gather(x, axis):
    count = lax.axis_size(axis)
    spread = jnp.broadcast_to(x[None], (count,) + x.shape)
    return lax.all_to_all(spread, axis, 0, 0, tiled=True)


def a2a_scatter_sum(x, axis):
    return lax.all_to_all(x, axis, 0, 0, tiled=True).sum(axis=0)


def block_partial(query, query_rope, keys_lat, keys_rope, valid):
    scale = QK ** (-0.5)
    scores = (
        jnp.einsum("rmc,rkc->rmk", query, keys_lat, preferred_element_type=jnp.float32)
        + jnp.einsum("rmc,rkc->rmk", query_rope, keys_rope, preferred_element_type=jnp.float32)
    ) * scale
    masked = jnp.where(valid, scores, NEG_FILL)
    peak_val = jnp.max(masked, axis=2)
    weights = jnp.where(valid, jnp.exp(masked - peak_val[:, :, None]), 0.0)
    weight_sum = jnp.sum(weights, axis=2)
    summed = jnp.einsum(
        "rmk,rkc->rmc", weights.astype(jnp.bfloat16), keys_lat, preferred_element_type=jnp.float32
    )
    return (peak_val, weight_sum, summed)


def merge_pair(left_part, right_part):
    peak_left, total_left, sum_left = left_part
    peak_right, total_right, sum_right = right_part
    peak_val = jnp.maximum(peak_left, peak_right)
    factor_left = jnp.exp(peak_left - peak_val)
    factor_right = jnp.exp(peak_right - peak_val)
    weight_sum = factor_left * total_left + factor_right * total_right
    summed = factor_left[..., None] * sum_left + factor_right[..., None] * sum_right
    return (peak_val, weight_sum, summed)


def local(
    hidden_in,
    q_lat,
    q_rope,
    new_lat,
    new_rope,
    cache_lat,
    cache_rope,
    lengths,
    w_uv,
    w_out,
    norm_gain,
    w_router,
    routes,
    w_gate,
    w_up,
    w_down,
):
    requests, new_steps, head_count, latent_dim = q_lat.shape
    me = lax.axis_index("blk")
    blk_bits = lax.axis_size("blk").bit_length() - 1
    exp_bits = lax.axis_size("exp").bit_length() - 1
    query_rows = new_steps * head_count
    query = q_lat.reshape(requests, query_rows, latent_dim)
    query_rope = q_rope.reshape(requests, query_rows, q_rope.shape[3])
    cache_span = cache_lat.shape[1]
    position = me * cache_span + lax.iota(jnp.int32, cache_span)
    cache_valid = jnp.broadcast_to(
        position[None, None, :] < lengths[:, None, None], (requests, query_rows, cache_span)
    )
    peak_val, weight_sum, summed = block_partial(query, query_rope, cache_lat, cache_rope, cache_valid)
    head_bits = head_count.bit_length() - 1
    split = (2,) * head_bits
    state = (
        peak_val.reshape(requests, new_steps, head_count).transpose(2, 0, 1).reshape(split + (requests, new_steps)),
        weight_sum.reshape(requests, new_steps, head_count).transpose(2, 0, 1).reshape(split + (requests, new_steps)),
        summed.reshape(requests, new_steps, head_count, latent_dim)
        .transpose(2, 0, 1, 3)
        .reshape(split + (requests, new_steps, latent_dim)),
    )
    low_bits = blk_bits - head_bits
    order = [head_bits - 1] + list(range(head_bits - 1))
    remaining = list(range(head_bits - 1, -1, -1))
    for head_bit in order:
        axis_pos = remaining.index(head_bit)
        remaining.pop(axis_pos)
        bit = head_bit + low_bits
        side = (me >> bit) & 1
        keep = jax.tree.map(lambda part: lax.dynamic_index_in_dim(part, side, axis_pos, keepdims=False), state)
        send = jax.tree.map(lambda part: lax.dynamic_index_in_dim(part, 1 - side, axis_pos, keepdims=False), state)
        state = merge_pair(keep, exchange_state(send, "blk", 1 << bit))
    for bit in range(low_bits - 1, -1, -1):
        state = merge_pair(state, exchange_state(state, "blk", 1 << bit))
    head_pick = me >> low_bits
    own_query = lax.dynamic_index_in_dim(q_lat, head_pick, axis=2, keepdims=False)
    own_rope = lax.dynamic_index_in_dim(q_rope, head_pick, axis=2, keepdims=False)
    fresh_valid = lax.iota(jnp.int32, new_steps)[None, :] <= lax.iota(jnp.int32, new_steps)[:, None]
    fresh_valid = jnp.broadcast_to(fresh_valid[None, :, :], (requests, new_steps, new_steps))
    fresh_part = block_partial(own_query, own_rope, new_lat, new_rope, fresh_valid)
    peak_val, weight_sum, summed = merge_pair(state, fresh_part)
    lat_out = (summed / weight_sum[:, :, None]).astype(jnp.bfloat16)
    token_rows = requests * new_steps
    lat_head = lat_out.reshape(token_rows, latent_dim)
    heads_out = jnp.dot(lat_head, w_uv, preferred_element_type=jnp.float32).astype(jnp.bfloat16)
    proj_part = jnp.dot(heads_out, w_out, preferred_element_type=jnp.float32)
    projected = a2a_sum(proj_part, "blk")
    width = hidden_in.shape[2]
    mixed = hidden_in.reshape(token_rows, width).astype(jnp.float32) + projected
    meansq = jnp.mean(mixed * mixed, axis=1, keepdims=True)
    normed = (mixed * lax.rsqrt(meansq + NORM_EPS) * norm_gain[None, :]).astype(jnp.bfloat16)
    affinity = jax.nn.sigmoid(jnp.dot(normed, w_router, preferred_element_type=jnp.float32))
    expert_total = w_router.shape[1]
    top_count = routes.shape[2]
    flat_routes = routes.reshape(token_rows, top_count)
    route_hits = flat_routes[:, :, None] == lax.iota(jnp.int32, expert_total)[None, None, :]
    chosen = jnp.sum(jnp.where(route_hits, affinity[:, None, :], 0.0), axis=2)
    route_weight = ROUTE_SCALE * chosen / jnp.sum(chosen, axis=1, keepdims=True)
    local_count = w_gate.shape[0]
    local_ids = me * local_count + lax.iota(jnp.int32, local_count)
    pair_routes = flat_routes.reshape(token_rows * top_count)
    local_hits = (pair_routes[:, None] == local_ids[None, :]).astype(jnp.int32)
    ranks = jnp.cumsum(local_hits, axis=0) - 1
    slot_ids = lax.iota(jnp.int32, CAP)
    slot_match = local_hits.T[:, None, :] * (ranks.T[:, None, :] == slot_ids[None, :, None]).astype(
        jnp.int32
    )
    select = slot_match.reshape(local_count, CAP, token_rows, top_count).astype(jnp.float32)
    dispatch_map = jnp.sum(select, axis=3)
    combine_map = jnp.sum(select * route_weight[None, None, :, :], axis=3)
    dispatched = jnp.einsum(
        "esr,rd->esd", dispatch_map.astype(jnp.bfloat16), normed, preferred_element_type=jnp.float32
    ).astype(jnp.bfloat16)
    gathered = a2a_gather(dispatched, "exp")
    groups = gathered.shape[0]
    piece = gathered.transpose(1, 0, 2, 3).reshape(local_count, groups * CAP, width)
    gate = jnp.einsum("erd,edf->erf", piece, w_gate, preferred_element_type=jnp.float32)
    upper = jnp.einsum("erd,edf->erf", piece, w_up, preferred_element_type=jnp.float32)
    hidden_all = (jax.nn.silu(gate) * upper).astype(jnp.bfloat16)
    partial_out = jnp.einsum("erf,efd->erd", hidden_all, w_down, preferred_element_type=jnp.float32)
    groups_out = partial_out.reshape(local_count, groups, CAP, width).transpose(1, 0, 2, 3)
    expert_out = a2a_scatter_sum(groups_out, "exp")
    moe_part = jnp.einsum("esr,esd->rd", combine_map, expert_out, precision=lax.Precision.HIGHEST)
    moe_all = a2a_sum(moe_part, "blk")
    result = (mixed + moe_all).astype(jnp.bfloat16)
    return result.reshape(requests, new_steps, width)


def solution(mesh):
    in_specs = (
        P("exp", None, None),
        P("exp", None, None, None),
        P("exp", None, None, None),
        P("exp", None, None),
        P("exp", None, None),
        P("exp", "blk", None),
        P("exp", "blk", None),
        P("exp"),
        P(None, "blk"),
        P("blk", None),
        P(),
        P(),
        P("exp", None, None),
        P("blk", None, "exp"),
        P("blk", None, "exp"),
        P("blk", "exp", None),
    )
    out_specs = P("exp", None, None)
    return jax.shard_map(local, mesh=mesh, in_specs=in_specs, out_specs=out_specs, check_vma=False)
```

```python
import jax
import jax.numpy as jnp
from jax import lax
from jax.sharding import PartitionSpec as P

V = 128
QK = 192
CAP = 3


NEG_FILL = -1e30
ROUTE_SCALE = 2.446
NORM_EPS = 1e-06


def xor_pairs(count, mask):
    return [(i, i ^ mask) for i in range(count)]


def exchange(x, axis, mask):
    count = lax.axis_size(axis)
    return jax.tree.map(lambda part: lax.ppermute(part, axis, xor_pairs(count, mask)), x)


def exchange_state(state, axis, mask):
    peak_val, weight_sum, summed = state
    packed = jnp.concatenate([summed, peak_val[..., None], weight_sum[..., None]], axis=-1)
    got = exchange(packed, axis, mask)
    width = summed.shape[-1]
    return (got[..., width], got[..., width + 1], got[..., :width])


def butterfly_sum(x, axis, bits):
    for bit in bits:
        x = x + exchange(x, axis, 1 << bit)
    return x


def butterfly_gather(x, axis, bits):
    me = lax.axis_index(axis)
    x = x[None]
    for bit in bits:
        other = exchange(x, axis, 1 << bit)
        high = ((me >> bit) & 1) == 1
        low_part = jnp.where(high, other, x)
        high_part = jnp.where(high, x, other)
        x = jnp.concatenate([low_part, high_part], axis=0)
    return x


def butterfly_scatter_sum(x, axis, bits):
    me = lax.axis_index(axis)
    for bit in bits:
        side = (me >> bit) & 1
        keep = lax.dynamic_index_in_dim(x, side, 0, keepdims=False)
        send = lax.dynamic_index_in_dim(x, 1 - side, 0, keepdims=False)
        x = keep + exchange(send, axis, 1 << bit)
    return x


def a2a_sum(x, axis):
    count = lax.axis_size(axis)
    rows, cols = x.shape
    parts = x.reshape(rows, count, cols // count).transpose(1, 0, 2)
    mine = lax.all_to_all(parts, axis, 0, 0, tiled=True).sum(axis=0)
    spread = jnp.broadcast_to(mine[None], (count,) + mine.shape)
    back = lax.all_to_all(spread, axis, 0, 0, tiled=True)
    return back.transpose(1, 0, 2).reshape(rows, cols)


def a2a_gather(x, axis):
    count = lax.axis_size(axis)
    spread = jnp.broadcast_to(x[None], (count,) + x.shape)
    return lax.all_to_all(spread, axis, 0, 0, tiled=True)


def a2a_scatter_sum(x, axis):
    return lax.all_to_all(x, axis, 0, 0, tiled=True).sum(axis=0)


def block_partial(query, query_rope, keys_lat, keys_rope, valid):
    scale = QK ** (-0.5)
    scores = (
        jnp.einsum("rmc,rkc->rmk", query, keys_lat, preferred_element_type=jnp.float32)
        + jnp.einsum("rmc,rkc->rmk", query_rope, keys_rope, preferred_element_type=jnp.float32)
    ) * scale
    masked = jnp.where(valid, scores, NEG_FILL)
    peak_val = jnp.max(masked, axis=2)
    weights = jnp.where(valid, jnp.exp(masked - peak_val[:, :, None]), 0.0)
    weight_sum = jnp.sum(weights, axis=2)
    summed = jnp.einsum(
        "rmk,rkc->rmc", weights.astype(jnp.bfloat16), keys_lat, preferred_element_type=jnp.float32
    )
    return (peak_val, weight_sum, summed)


def merge_pair(left_part, right_part):
    peak_left, total_left, sum_left = left_part
    peak_right, total_right, sum_right = right_part
    peak_val = jnp.maximum(peak_left, peak_right)
    factor_left = jnp.exp(peak_left - peak_val)
    factor_right = jnp.exp(peak_right - peak_val)
    weight_sum = factor_left * total_left + factor_right * total_right
    summed = factor_left[..., None] * sum_left + factor_right[..., None] * sum_right
    return (peak_val, weight_sum, summed)


def local(
    hidden_in,
    q_lat,
    q_rope,
    new_lat,
    new_rope,
    cache_lat,
    cache_rope,
    lengths,
    w_uv,
    w_out,
    norm_gain,
    w_router,
    routes,
    w_gate,
    w_up,
    w_down,
):
    requests, new_steps, head_count, latent_dim = q_lat.shape
    me = lax.axis_index("blk")
    blk_bits = lax.axis_size("blk").bit_length() - 1
    exp_bits = lax.axis_size("exp").bit_length() - 1
    query_rows = new_steps * head_count
    query = q_lat.reshape(requests, query_rows, latent_dim)
    query_rope = q_rope.reshape(requests, query_rows, q_rope.shape[3])
    cache_span = cache_lat.shape[1]
    position = me * cache_span + lax.iota(jnp.int32, cache_span)
    cache_valid = jnp.broadcast_to(
        position[None, None, :] < lengths[:, None, None], (requests, query_rows, cache_span)
    )
    peak_val, weight_sum, summed = block_partial(query, query_rope, cache_lat, cache_rope, cache_valid)
    head_bits = head_count.bit_length() - 1
    low_bits = blk_bits - head_bits
    packed = jnp.concatenate([summed, peak_val[..., None], weight_sum[..., None]], axis=-1)
    packed = packed.reshape(requests, new_steps, head_count, latent_dim + 2).transpose(2, 0, 1, 3)
    packed = packed.reshape(head_count * requests, new_steps, latent_dim + 2)
    got = lax.all_to_all(packed, "blk", 0, 0, tiled=True)
    peaks = got[..., latent_dim]
    totals = got[..., latent_dim + 1]
    peak_all = jnp.max(peaks, axis=0)
    factors = jnp.exp(peaks - peak_all[None])
    state = (
        peak_all[None],
        jnp.sum(factors * totals, axis=0)[None],
        jnp.sum(factors[..., None] * got[..., :latent_dim], axis=0)[None],
    )
    head_pick = me >> low_bits
    request_pick = me & ((1 << low_bits) - 1)
    own_query = lax.dynamic_index_in_dim(q_lat, request_pick, axis=0, keepdims=True)
    own_query = lax.dynamic_index_in_dim(own_query, head_pick, axis=2, keepdims=False)
    own_rope = lax.dynamic_index_in_dim(q_rope, request_pick, axis=0, keepdims=True)
    own_rope = lax.dynamic_index_in_dim(own_rope, head_pick, axis=2, keepdims=False)
    own_lat = lax.dynamic_index_in_dim(new_lat, request_pick, axis=0, keepdims=True)
    own_new_rope = lax.dynamic_index_in_dim(new_rope, request_pick, axis=0, keepdims=True)
    fresh_valid = lax.iota(jnp.int32, new_steps)[None, :] <= lax.iota(jnp.int32, new_steps)[:, None]
    fresh_valid = fresh_valid[None, :, :]
    fresh_part = block_partial(own_query, own_rope, own_lat, own_new_rope, fresh_valid)
    peak_val, weight_sum, summed = merge_pair(state, fresh_part)
    own_out = (summed / weight_sum[:, :, None]).astype(jnp.bfloat16)
    lat_out = butterfly_gather(own_out[0], "blk", range(low_bits))
    token_rows = requests * new_steps
    lat_head = lat_out.reshape(token_rows, latent_dim)
    heads_out = jnp.dot(lat_head, w_uv, preferred_element_type=jnp.float32).astype(jnp.bfloat16)
    proj_part = jnp.dot(heads_out, w_out, preferred_element_type=jnp.float32)
    projected = a2a_sum(proj_part, "blk")
    width = hidden_in.shape[2]
    mixed = hidden_in.reshape(token_rows, width).astype(jnp.float32) + projected
    meansq = jnp.mean(mixed * mixed, axis=1, keepdims=True)
    normed = (mixed * lax.rsqrt(meansq + NORM_EPS) * norm_gain[None, :]).astype(jnp.bfloat16)
    affinity = jax.nn.sigmoid(jnp.dot(normed, w_router, preferred_element_type=jnp.float32))
    expert_total = w_router.shape[1]
    top_count = routes.shape[2]
    flat_routes = routes.reshape(token_rows, top_count)
    route_hits = flat_routes[:, :, None] == lax.iota(jnp.int32, expert_total)[None, None, :]
    chosen = jnp.sum(jnp.where(route_hits, affinity[:, None, :], 0.0), axis=2)
    route_weight = ROUTE_SCALE * chosen / jnp.sum(chosen, axis=1, keepdims=True)
    local_count = w_gate.shape[0]
    local_ids = me * local_count + lax.iota(jnp.int32, local_count)
    pair_routes = flat_routes.reshape(token_rows * top_count)
    local_hits = (pair_routes[:, None] == local_ids[None, :]).astype(jnp.int32)
    ranks = jnp.cumsum(local_hits, axis=0) - 1
    slot_ids = lax.iota(jnp.int32, CAP)
    slot_match = local_hits.T[:, None, :] * (ranks.T[:, None, :] == slot_ids[None, :, None]).astype(
        jnp.int32
    )
    select = slot_match.reshape(local_count, CAP, token_rows, top_count).astype(jnp.float32)
    dispatch_map = jnp.sum(select, axis=3)
    combine_map = jnp.sum(select * route_weight[None, None, :, :], axis=3)
    dispatched = jnp.einsum(
        "esr,rd->esd", dispatch_map.astype(jnp.bfloat16), normed, preferred_element_type=jnp.float32
    ).astype(jnp.bfloat16)
    gathered = a2a_gather(dispatched, "exp")
    groups = gathered.shape[0]
    piece = gathered.transpose(1, 0, 2, 3).reshape(local_count, groups * CAP, width)
    gate = jnp.einsum("erd,edf->erf", piece, w_gate, preferred_element_type=jnp.float32)
    upper = jnp.einsum("erd,edf->erf", piece, w_up, preferred_element_type=jnp.float32)
    hidden_all = (jax.nn.silu(gate) * upper).astype(jnp.bfloat16)
    partial_out = jnp.einsum("erf,efd->erd", hidden_all, w_down, preferred_element_type=jnp.float32)
    groups_out = partial_out.reshape(local_count, groups, CAP, width).transpose(1, 0, 2, 3)
    expert_out = a2a_scatter_sum(groups_out, "exp")
    moe_part = jnp.einsum("esr,esd->rd", combine_map, expert_out, precision=lax.Precision.HIGHEST)
    moe_all = a2a_sum(moe_part, "blk")
    result = (mixed + moe_all).astype(jnp.bfloat16)
    return result.reshape(requests, new_steps, width)


def solution(mesh):
    in_specs = (
        P("exp", None, None),
        P("exp", None, None, None),
        P("exp", None, None, None),
        P("exp", None, None),
        P("exp", None, None),
        P("exp", "blk", None),
        P("exp", "blk", None),
        P("exp"),
        P(None, "blk"),
        P("blk", None),
        P(),
        P(),
        P("exp", None, None),
        P("blk", None, "exp"),
        P("blk", None, "exp"),
        P("blk", "exp", None),
    )
    out_specs = P("exp", None, None)
    return jax.shard_map(local, mesh=mesh, in_specs=in_specs, out_specs=out_specs, check_vma=False)
```

```python
import jax
import jax.numpy as jnp
from jax import lax
from jax.sharding import PartitionSpec as P

V = 128
QK = 192
CAP = 3


NEG_FILL = -1e30
ROUTE_SCALE = 2.446
NORM_EPS = 1e-06


def xor_pairs(count, mask):
    return [(i, i ^ mask) for i in range(count)]


def exchange(x, axis, mask):
    count = lax.axis_size(axis)
    return jax.tree.map(lambda part: lax.ppermute(part, axis, xor_pairs(count, mask)), x)


def exchange_state(state, axis, mask):
    peak_val, weight_sum, summed = state
    packed = jnp.concatenate([summed, peak_val[..., None], weight_sum[..., None]], axis=-1)
    got = exchange(packed, axis, mask)
    width = summed.shape[-1]
    return (got[..., width], got[..., width + 1], got[..., :width])


def butterfly_sum(x, axis, bits):
    for bit in bits:
        x = x + exchange(x, axis, 1 << bit)
    return x


def butterfly_gather(x, axis, bits):
    me = lax.axis_index(axis)
    x = x[None]
    for bit in bits:
        other = exchange(x, axis, 1 << bit)
        high = ((me >> bit) & 1) == 1
        low_part = jnp.where(high, other, x)
        high_part = jnp.where(high, x, other)
        x = jnp.concatenate([low_part, high_part], axis=0)
    return x


def butterfly_scatter_sum(x, axis, bits):
    me = lax.axis_index(axis)
    for bit in bits:
        side = (me >> bit) & 1
        keep = lax.dynamic_index_in_dim(x, side, 0, keepdims=False)
        send = lax.dynamic_index_in_dim(x, 1 - side, 0, keepdims=False)
        x = keep + exchange(send, axis, 1 << bit)
    return x


def a2a_sum(x, axis):
    count = lax.axis_size(axis)
    rows, cols = x.shape
    parts = x.reshape(rows, count, cols // count).transpose(1, 0, 2).astype(jnp.bfloat16)
    mine = lax.all_to_all(parts, axis, 0, 0, tiled=True).astype(jnp.float32).sum(axis=0)
    spread = jnp.broadcast_to(mine[None], (count,) + mine.shape)
    back = lax.all_to_all(spread, axis, 0, 0, tiled=True)
    return back.transpose(1, 0, 2).reshape(rows, cols)


def a2a_gather(x, axis):
    count = lax.axis_size(axis)
    spread = jnp.broadcast_to(x[None], (count,) + x.shape)
    return lax.all_to_all(spread, axis, 0, 0, tiled=True)


def a2a_scatter_sum(x, axis):
    got = lax.all_to_all(x.astype(jnp.bfloat16), axis, 0, 0, tiled=True)
    return got.astype(jnp.float32).sum(axis=0)


def block_partial(query, query_rope, keys_lat, keys_rope, valid):
    scale = QK ** (-0.5)
    scores = (
        jnp.einsum("rmc,rkc->rmk", query, keys_lat, preferred_element_type=jnp.float32)
        + jnp.einsum("rmc,rkc->rmk", query_rope, keys_rope, preferred_element_type=jnp.float32)
    ) * scale
    masked = jnp.where(valid, scores, NEG_FILL)
    peak_val = jnp.max(masked, axis=2)
    weights = jnp.where(valid, jnp.exp(masked - peak_val[:, :, None]), 0.0)
    weight_sum = jnp.sum(weights, axis=2)
    summed = jnp.einsum(
        "rmk,rkc->rmc", weights.astype(jnp.bfloat16), keys_lat, preferred_element_type=jnp.float32
    )
    return (peak_val, weight_sum, summed)


def merge_pair(left_part, right_part):
    peak_left, total_left, sum_left = left_part
    peak_right, total_right, sum_right = right_part
    peak_val = jnp.maximum(peak_left, peak_right)
    factor_left = jnp.exp(peak_left - peak_val)
    factor_right = jnp.exp(peak_right - peak_val)
    weight_sum = factor_left * total_left + factor_right * total_right
    summed = factor_left[..., None] * sum_left + factor_right[..., None] * sum_right
    return (peak_val, weight_sum, summed)


def local(
    hidden_in,
    q_lat,
    q_rope,
    new_lat,
    new_rope,
    cache_lat,
    cache_rope,
    lengths,
    w_uv,
    w_out,
    norm_gain,
    w_router,
    routes,
    w_gate,
    w_up,
    w_down,
):
    requests, new_steps, head_count, latent_dim = q_lat.shape
    me = lax.axis_index("blk")
    blk_bits = lax.axis_size("blk").bit_length() - 1
    exp_bits = lax.axis_size("exp").bit_length() - 1
    query_rows = new_steps * head_count
    query = q_lat.reshape(requests, query_rows, latent_dim)
    query_rope = q_rope.reshape(requests, query_rows, q_rope.shape[3])
    cache_span = cache_lat.shape[1]
    position = me * cache_span + lax.iota(jnp.int32, cache_span)
    cache_valid = jnp.broadcast_to(
        position[None, None, :] < lengths[:, None, None], (requests, query_rows, cache_span)
    )
    peak_val, weight_sum, summed = block_partial(query, query_rope, cache_lat, cache_rope, cache_valid)
    head_bits = head_count.bit_length() - 1
    low_bits = blk_bits - head_bits
    stats = jnp.stack([peak_val, weight_sum], axis=-1)
    stats = stats.reshape(requests, new_steps, head_count, 2).transpose(2, 0, 1, 3)
    stats = lax.all_to_all(stats.reshape(head_count * requests, new_steps, 2), "blk", 0, 0, tiled=True)
    sums = summed.astype(jnp.bfloat16).reshape(requests, new_steps, head_count, latent_dim).transpose(2, 0, 1, 3)
    sums = lax.all_to_all(sums.reshape(head_count * requests, new_steps, latent_dim), "blk", 0, 0, tiled=True)
    peaks = stats[..., 0]
    totals = stats[..., 1]
    peak_all = jnp.max(peaks, axis=0)
    factors = jnp.exp(peaks - peak_all[None])
    state = (
        peak_all[None],
        jnp.sum(factors * totals, axis=0)[None],
        jnp.sum(factors[..., None] * sums.astype(jnp.float32), axis=0)[None],
    )
    head_pick = me >> low_bits
    request_pick = me & ((1 << low_bits) - 1)
    own_query = lax.dynamic_index_in_dim(q_lat, request_pick, axis=0, keepdims=True)
    own_query = lax.dynamic_index_in_dim(own_query, head_pick, axis=2, keepdims=False)
    own_rope = lax.dynamic_index_in_dim(q_rope, request_pick, axis=0, keepdims=True)
    own_rope = lax.dynamic_index_in_dim(own_rope, head_pick, axis=2, keepdims=False)
    own_lat = lax.dynamic_index_in_dim(new_lat, request_pick, axis=0, keepdims=True)
    own_new_rope = lax.dynamic_index_in_dim(new_rope, request_pick, axis=0, keepdims=True)
    fresh_valid = lax.iota(jnp.int32, new_steps)[None, :] <= lax.iota(jnp.int32, new_steps)[:, None]
    fresh_valid = fresh_valid[None, :, :]
    fresh_part = block_partial(own_query, own_rope, own_lat, own_new_rope, fresh_valid)
    peak_val, weight_sum, summed = merge_pair(state, fresh_part)
    own_out = (summed / weight_sum[:, :, None]).astype(jnp.bfloat16)
    lat_out = butterfly_gather(own_out[0], "blk", range(low_bits))
    token_rows = requests * new_steps
    lat_head = lat_out.reshape(token_rows, latent_dim)
    heads_out = jnp.dot(lat_head, w_uv, preferred_element_type=jnp.float32).astype(jnp.bfloat16)
    proj_part = jnp.dot(heads_out, w_out, preferred_element_type=jnp.float32)
    projected = a2a_sum(proj_part, "blk")
    width = hidden_in.shape[2]
    mixed = hidden_in.reshape(token_rows, width).astype(jnp.float32) + projected
    meansq = jnp.mean(mixed * mixed, axis=1, keepdims=True)
    normed = (mixed * lax.rsqrt(meansq + NORM_EPS) * norm_gain[None, :]).astype(jnp.bfloat16)
    affinity = jax.nn.sigmoid(jnp.dot(normed, w_router, preferred_element_type=jnp.float32))
    expert_total = w_router.shape[1]
    top_count = routes.shape[2]
    flat_routes = routes.reshape(token_rows, top_count)
    route_hits = flat_routes[:, :, None] == lax.iota(jnp.int32, expert_total)[None, None, :]
    chosen = jnp.sum(jnp.where(route_hits, affinity[:, None, :], 0.0), axis=2)
    route_weight = ROUTE_SCALE * chosen / jnp.sum(chosen, axis=1, keepdims=True)
    local_count = w_gate.shape[0]
    local_ids = me * local_count + lax.iota(jnp.int32, local_count)
    pair_routes = flat_routes.reshape(token_rows * top_count)
    local_hits = (pair_routes[:, None] == local_ids[None, :]).astype(jnp.int32)
    ranks = jnp.cumsum(local_hits, axis=0) - 1
    slot_ids = lax.iota(jnp.int32, CAP)
    slot_match = local_hits.T[:, None, :] * (ranks.T[:, None, :] == slot_ids[None, :, None]).astype(
        jnp.int32
    )
    select = slot_match.reshape(local_count, CAP, token_rows, top_count).astype(jnp.float32)
    dispatch_map = jnp.sum(select, axis=3)
    combine_map = jnp.sum(select * route_weight[None, None, :, :], axis=3)
    dispatched = jnp.einsum(
        "esr,rd->esd", dispatch_map.astype(jnp.bfloat16), normed, preferred_element_type=jnp.float32
    ).astype(jnp.bfloat16)
    gathered = a2a_gather(dispatched, "exp")
    groups = gathered.shape[0]
    piece = gathered.transpose(1, 0, 2, 3).reshape(local_count, groups * CAP, width)
    gate = jnp.einsum("erd,edf->erf", piece, w_gate, preferred_element_type=jnp.float32)
    upper = jnp.einsum("erd,edf->erf", piece, w_up, preferred_element_type=jnp.float32)
    hidden_all = (jax.nn.silu(gate) * upper).astype(jnp.bfloat16)
    partial_out = jnp.einsum("erf,efd->erd", hidden_all, w_down, preferred_element_type=jnp.float32)
    groups_out = partial_out.reshape(local_count, groups, CAP, width).transpose(1, 0, 2, 3)
    expert_out = a2a_scatter_sum(groups_out, "exp")
    moe_part = jnp.einsum("esr,esd->rd", combine_map, expert_out, precision=lax.Precision.HIGHEST)
    moe_all = a2a_sum(moe_part, "blk")
    result = (mixed + moe_all).astype(jnp.bfloat16)
    return result.reshape(requests, new_steps, width)


def solution(mesh):
    in_specs = (
        P("exp", None, None),
        P("exp", None, None, None),
        P("exp", None, None, None),
        P("exp", None, None),
        P("exp", None, None),
        P("exp", "blk", None),
        P("exp", "blk", None),
        P("exp"),
        P(None, "blk"),
        P("blk", None),
        P(),
        P(),
        P("exp", None, None),
        P("blk", None, "exp"),
        P("blk", None, "exp"),
        P("blk", "exp", None),
    )
    out_specs = P("exp", None, None)
    return jax.shard_map(local, mesh=mesh, in_specs=in_specs, out_specs=out_specs, check_vma=False)
```

```python
import jax
import jax.numpy as jnp
from jax import lax
from jax.sharding import PartitionSpec as P

V = 128
QK = 192
CAP = 3


NEG_FILL = -1e30
ROUTE_SCALE = 2.446
NORM_EPS = 1e-06


def xor_pairs(count, mask):
    return [(i, i ^ mask) for i in range(count)]


def exchange(x, axis, mask):
    count = lax.axis_size(axis)
    return jax.tree.map(lambda part: lax.ppermute(part, axis, xor_pairs(count, mask)), x)


def exchange_state(state, axis, mask):
    peak_val, weight_sum, summed = state
    packed = jnp.concatenate([summed, peak_val[..., None], weight_sum[..., None]], axis=-1)
    got = exchange(packed, axis, mask)
    width = summed.shape[-1]
    return (got[..., width], got[..., width + 1], got[..., :width])


def butterfly_sum(x, axis, bits):
    for bit in bits:
        x = x + exchange(x, axis, 1 << bit)
    return x


def butterfly_gather(x, axis, bits):
    me = lax.axis_index(axis)
    x = x[None]
    for bit in bits:
        other = exchange(x, axis, 1 << bit)
        high = ((me >> bit) & 1) == 1
        low_part = jnp.where(high, other, x)
        high_part = jnp.where(high, x, other)
        x = jnp.concatenate([low_part, high_part], axis=0)
    return x


def butterfly_scatter_sum(x, axis, bits):
    me = lax.axis_index(axis)
    for bit in bits:
        side = (me >> bit) & 1
        keep = lax.dynamic_index_in_dim(x, side, 0, keepdims=False)
        send = lax.dynamic_index_in_dim(x, 1 - side, 0, keepdims=False)
        x = keep + exchange(send, axis, 1 << bit)
    return x


def a2a_sum(x, axis):
    count = lax.axis_size(axis)
    rows, cols = x.shape
    parts = x.reshape(rows, count, cols // count).transpose(1, 0, 2).astype(jnp.bfloat16)
    mine = lax.all_to_all(parts, axis, 0, 0, tiled=True).astype(jnp.float32).sum(axis=0)
    spread = jnp.broadcast_to(mine[None], (count,) + mine.shape)
    back = lax.all_to_all(spread, axis, 0, 0, tiled=True)
    return back.transpose(1, 0, 2).reshape(rows, cols)


def a2a_gather(x, axis):
    count = lax.axis_size(axis)
    spread = jnp.broadcast_to(x[None], (count,) + x.shape)
    return lax.all_to_all(spread, axis, 0, 0, tiled=True)


def a2a_scatter_sum(x, axis):
    got = lax.all_to_all(x.astype(jnp.bfloat16), axis, 0, 0, tiled=True)
    return got.astype(jnp.float32).sum(axis=0)


def block_partial(query, query_rope, keys_lat, keys_rope, valid):
    scale = QK ** (-0.5)
    scores = (
        jnp.einsum("rmc,rkc->rmk", query, keys_lat, preferred_element_type=jnp.float32)
        + jnp.einsum("rmc,rkc->rmk", query_rope, keys_rope, preferred_element_type=jnp.float32)
    ) * scale
    masked = jnp.where(valid, scores, NEG_FILL)
    peak_val = jnp.max(masked, axis=2)
    weights = jnp.where(valid, jnp.exp(masked - peak_val[:, :, None]), 0.0)
    weight_sum = jnp.sum(weights, axis=2)
    summed = jnp.einsum(
        "rmk,rkc->rmc", weights.astype(jnp.bfloat16), keys_lat, preferred_element_type=jnp.float32
    )
    return (peak_val, weight_sum, summed)


def merge_pair(left_part, right_part):
    peak_left, total_left, sum_left = left_part
    peak_right, total_right, sum_right = right_part
    peak_val = jnp.maximum(peak_left, peak_right)
    factor_left = jnp.exp(peak_left - peak_val)
    factor_right = jnp.exp(peak_right - peak_val)
    weight_sum = factor_left * total_left + factor_right * total_right
    summed = factor_left[..., None] * sum_left + factor_right[..., None] * sum_right
    return (peak_val, weight_sum, summed)


def local(
    hidden_in,
    q_lat,
    q_rope,
    new_lat,
    new_rope,
    cache_lat,
    cache_rope,
    lengths,
    w_uv,
    w_out,
    norm_gain,
    w_router,
    routes,
    w_gate,
    w_up,
    w_down,
):
    requests, new_steps, head_count, latent_dim = q_lat.shape
    me = lax.axis_index("blk")
    blk_bits = lax.axis_size("blk").bit_length() - 1
    exp_bits = lax.axis_size("exp").bit_length() - 1
    query_rows = new_steps * head_count
    query = q_lat.reshape(requests, query_rows, latent_dim)
    query_rope = q_rope.reshape(requests, query_rows, q_rope.shape[3])
    cache_span = cache_lat.shape[1]
    position = me * cache_span + lax.iota(jnp.int32, cache_span)
    cache_valid = jnp.broadcast_to(
        position[None, None, :] < lengths[:, None, None], (requests, query_rows, cache_span)
    )
    peak_val, weight_sum, summed = block_partial(query, query_rope, cache_lat, cache_rope, cache_valid)
    head_bits = head_count.bit_length() - 1
    low_bits = blk_bits - head_bits
    packed = jnp.concatenate([summed, peak_val[..., None], weight_sum[..., None]], axis=-1)
    packed = packed.reshape(requests, new_steps, head_count, latent_dim + 2).transpose(2, 0, 1, 3)
    packed = packed.reshape(head_count * requests, new_steps, latent_dim + 2)
    got = lax.all_to_all(packed, "blk", 0, 0, tiled=True)
    peaks = got[..., latent_dim]
    totals = got[..., latent_dim + 1]
    peak_all = jnp.max(peaks, axis=0)
    factors = jnp.exp(peaks - peak_all[None])
    state = (
        peak_all[None],
        jnp.sum(factors * totals, axis=0)[None],
        jnp.sum(factors[..., None] * got[..., :latent_dim], axis=0)[None],
    )
    head_pick = me >> low_bits
    request_pick = me & ((1 << low_bits) - 1)
    own_query = lax.dynamic_index_in_dim(q_lat, request_pick, axis=0, keepdims=True)
    own_query = lax.dynamic_index_in_dim(own_query, head_pick, axis=2, keepdims=False)
    own_rope = lax.dynamic_index_in_dim(q_rope, request_pick, axis=0, keepdims=True)
    own_rope = lax.dynamic_index_in_dim(own_rope, head_pick, axis=2, keepdims=False)
    own_lat = lax.dynamic_index_in_dim(new_lat, request_pick, axis=0, keepdims=True)
    own_new_rope = lax.dynamic_index_in_dim(new_rope, request_pick, axis=0, keepdims=True)
    fresh_valid = lax.iota(jnp.int32, new_steps)[None, :] <= lax.iota(jnp.int32, new_steps)[:, None]
    fresh_valid = fresh_valid[None, :, :]
    fresh_part = block_partial(own_query, own_rope, own_lat, own_new_rope, fresh_valid)
    peak_val, weight_sum, summed = merge_pair(state, fresh_part)
    own_out = (summed / weight_sum[:, :, None]).astype(jnp.bfloat16)
    lat_out = butterfly_gather(own_out[0], "blk", range(low_bits))
    token_rows = requests * new_steps
    lat_head = lat_out.reshape(token_rows, latent_dim)
    heads_out = jnp.dot(lat_head, w_uv, preferred_element_type=jnp.float32).astype(jnp.bfloat16)
    proj_part = jnp.dot(heads_out, w_out, preferred_element_type=jnp.float32)
    projected = a2a_sum(proj_part, "blk")
    width = hidden_in.shape[2]
    mixed = hidden_in.reshape(token_rows, width).astype(jnp.float32) + projected
    meansq = jnp.mean(mixed * mixed, axis=1, keepdims=True)
    normed = (mixed * lax.rsqrt(meansq + NORM_EPS) * norm_gain[None, :]).astype(jnp.bfloat16)
    affinity = jax.nn.sigmoid(jnp.dot(normed, w_router, preferred_element_type=jnp.float32))
    expert_total = w_router.shape[1]
    top_count = routes.shape[2]
    flat_routes = routes.reshape(token_rows, top_count)
    route_hits = flat_routes[:, :, None] == lax.iota(jnp.int32, expert_total)[None, None, :]
    chosen = jnp.sum(jnp.where(route_hits, affinity[:, None, :], 0.0), axis=2)
    route_weight = ROUTE_SCALE * chosen / jnp.sum(chosen, axis=1, keepdims=True)
    local_count = w_gate.shape[0]
    local_ids = me * local_count + lax.iota(jnp.int32, local_count)
    pair_routes = flat_routes.reshape(token_rows * top_count)
    local_hits = (pair_routes[:, None] == local_ids[None, :]).astype(jnp.int32)
    ranks = jnp.cumsum(local_hits, axis=0) - 1
    slot_ids = lax.iota(jnp.int32, CAP)
    slot_match = local_hits.T[:, None, :] * (ranks.T[:, None, :] == slot_ids[None, :, None]).astype(
        jnp.int32
    )
    select = slot_match.reshape(local_count, CAP, token_rows, top_count).astype(jnp.float32)
    dispatch_map = jnp.sum(select, axis=3)
    combine_map = jnp.sum(select * route_weight[None, None, :, :], axis=3)
    dispatched = jnp.einsum(
        "esr,rd->esd", dispatch_map.astype(jnp.bfloat16), normed, preferred_element_type=jnp.float32
    ).astype(jnp.bfloat16)
    gathered = a2a_gather(dispatched, "exp")
    groups = gathered.shape[0]
    piece = gathered.transpose(1, 0, 2, 3).reshape(local_count, groups * CAP, width)
    gate = jnp.einsum("erd,edf->erf", piece, w_gate, preferred_element_type=jnp.float32)
    upper = jnp.einsum("erd,edf->erf", piece, w_up, preferred_element_type=jnp.float32)
    hidden_all = (jax.nn.silu(gate) * upper).astype(jnp.bfloat16)
    partial_out = jnp.einsum("erf,efd->erd", hidden_all, w_down, preferred_element_type=jnp.float32)
    groups_out = partial_out.reshape(local_count, groups, CAP, width).transpose(1, 0, 2, 3)
    expert_out = a2a_scatter_sum(groups_out, "exp")
    moe_part = jnp.einsum("esr,esd->rd", combine_map, expert_out, precision=lax.Precision.HIGHEST)
    moe_all = a2a_sum(moe_part, "blk")
    result = (mixed + moe_all).astype(jnp.bfloat16)
    return result.reshape(requests, new_steps, width)


def solution(mesh):
    in_specs = (
        P("exp", None, None),
        P("exp", None, None, None),
        P("exp", None, None, None),
        P("exp", None, None),
        P("exp", None, None),
        P("exp", "blk", None),
        P("exp", "blk", None),
        P("exp"),
        P(None, "blk"),
        P("blk", None),
        P(),
        P(),
        P("exp", None, None),
        P("blk", None, "exp"),
        P("blk", None, "exp"),
        P("blk", "exp", None),
    )
    out_specs = P("exp", None, None)
    return jax.shard_map(local, mesh=mesh, in_specs=in_specs, out_specs=out_specs, check_vma=False)
```

```python
import jax
import jax.numpy as jnp
from jax import lax
from jax.sharding import PartitionSpec as P

V = 128
QK = 192
CAP = 3


NEG_FILL = -1e30
ROUTE_SCALE = 2.446
NORM_EPS = 1e-06


def xor_pairs(count, mask):
    return [(i, i ^ mask) for i in range(count)]


def exchange(x, axis, mask):
    count = lax.axis_size(axis)
    return jax.tree.map(lambda part: lax.ppermute(part, axis, xor_pairs(count, mask)), x)


def exchange_state(state, axis, mask):
    peak_val, weight_sum, summed = state
    packed = jnp.concatenate([summed, peak_val[..., None], weight_sum[..., None]], axis=-1)
    got = exchange(packed, axis, mask)
    width = summed.shape[-1]
    return (got[..., width], got[..., width + 1], got[..., :width])


def butterfly_sum(x, axis, bits):
    for bit in bits:
        x = x + exchange(x, axis, 1 << bit)
    return x


def butterfly_gather(x, axis, bits):
    me = lax.axis_index(axis)
    x = x[None]
    for bit in bits:
        other = exchange(x, axis, 1 << bit)
        high = ((me >> bit) & 1) == 1
        low_part = jnp.where(high, other, x)
        high_part = jnp.where(high, x, other)
        x = jnp.concatenate([low_part, high_part], axis=0)
    return x


def butterfly_scatter_sum(x, axis, bits):
    me = lax.axis_index(axis)
    for bit in bits:
        side = (me >> bit) & 1
        keep = lax.dynamic_index_in_dim(x, side, 0, keepdims=False)
        send = lax.dynamic_index_in_dim(x, 1 - side, 0, keepdims=False)
        x = keep + exchange(send, axis, 1 << bit)
    return x


def a2a_sum(x, axis):
    count = lax.axis_size(axis)
    rows, cols = x.shape
    parts = x.reshape(rows, count, cols // count).transpose(1, 0, 2).astype(jnp.bfloat16)
    mine = lax.all_to_all(parts, axis, 0, 0, tiled=True).astype(jnp.float32).sum(axis=0)
    spread = jnp.broadcast_to(mine[None], (count,) + mine.shape)
    back = lax.all_to_all(spread, axis, 0, 0, tiled=True)
    return back.transpose(1, 0, 2).reshape(rows, cols)


def a2a_gather(x, axis):
    count = lax.axis_size(axis)
    spread = jnp.broadcast_to(x[None], (count,) + x.shape)
    return lax.all_to_all(spread, axis, 0, 0, tiled=True)


def a2a_scatter_sum(x, axis):
    got = lax.all_to_all(x.astype(jnp.bfloat16), axis, 0, 0, tiled=True)
    return got.astype(jnp.float32).sum(axis=0)


def block_partial(query, query_rope, keys_lat, keys_rope, valid):
    scale = QK ** (-0.5)
    scores = (
        jnp.einsum("rmc,rkc->rmk", query, keys_lat, preferred_element_type=jnp.float32)
        + jnp.einsum("rmc,rkc->rmk", query_rope, keys_rope, preferred_element_type=jnp.float32)
    ) * scale
    masked = jnp.where(valid, scores, NEG_FILL)
    peak_val = jnp.max(masked, axis=2)
    weights = jnp.where(valid, jnp.exp(masked - peak_val[:, :, None]), 0.0)
    weight_sum = jnp.sum(weights, axis=2)
    summed = jnp.einsum(
        "rmk,rkc->rmc", weights.astype(jnp.bfloat16), keys_lat, preferred_element_type=jnp.float32
    )
    return (peak_val, weight_sum, summed)


def merge_pair(left_part, right_part):
    peak_left, total_left, sum_left = left_part
    peak_right, total_right, sum_right = right_part
    peak_val = jnp.maximum(peak_left, peak_right)
    factor_left = jnp.exp(peak_left - peak_val)
    factor_right = jnp.exp(peak_right - peak_val)
    weight_sum = factor_left * total_left + factor_right * total_right
    summed = factor_left[..., None] * sum_left + factor_right[..., None] * sum_right
    return (peak_val, weight_sum, summed)


def local(
    hidden_in,
    q_lat,
    q_rope,
    new_lat,
    new_rope,
    cache_lat,
    cache_rope,
    lengths,
    w_uv,
    w_out,
    norm_gain,
    w_router,
    routes,
    w_gate,
    w_up,
    w_down,
):
    requests, new_steps, head_count, latent_dim = q_lat.shape
    me = lax.axis_index("blk")
    blk_bits = lax.axis_size("blk").bit_length() - 1
    exp_bits = lax.axis_size("exp").bit_length() - 1
    query_rows = new_steps * head_count
    query = q_lat.reshape(requests, query_rows, latent_dim)
    query_rope = q_rope.reshape(requests, query_rows, q_rope.shape[3])
    cache_span = cache_lat.shape[1]
    position = me * cache_span + lax.iota(jnp.int32, cache_span)
    cache_valid = jnp.broadcast_to(
        position[None, None, :] < lengths[:, None, None], (requests, query_rows, cache_span)
    )
    peak_val, weight_sum, summed = block_partial(query, query_rope, cache_lat, cache_rope, cache_valid)
    head_bits = head_count.bit_length() - 1
    low_bits = blk_bits - head_bits
    packed = jnp.concatenate([summed, peak_val[..., None], weight_sum[..., None]], axis=-1)
    packed = packed.reshape(requests, new_steps, head_count, latent_dim + 2).transpose(2, 0, 1, 3)
    packed = packed.reshape(head_count * requests, new_steps, latent_dim + 2)
    flat = packed.reshape(head_count * requests, new_steps * (latent_dim + 2))
    got = lax.all_to_all(flat, "blk", 0, 0, tiled=True).reshape(packed.shape)
    peaks = got[..., latent_dim]
    totals = got[..., latent_dim + 1]
    peak_all = jnp.max(peaks, axis=0)
    factors = jnp.exp(peaks - peak_all[None])
    state = (
        peak_all[None],
        jnp.sum(factors * totals, axis=0)[None],
        jnp.sum(factors[..., None] * got[..., :latent_dim], axis=0)[None],
    )
    head_pick = me >> low_bits
    request_pick = me & ((1 << low_bits) - 1)
    own_query = lax.dynamic_index_in_dim(q_lat, request_pick, axis=0, keepdims=True)
    own_query = lax.dynamic_index_in_dim(own_query, head_pick, axis=2, keepdims=False)
    own_rope = lax.dynamic_index_in_dim(q_rope, request_pick, axis=0, keepdims=True)
    own_rope = lax.dynamic_index_in_dim(own_rope, head_pick, axis=2, keepdims=False)
    own_lat = lax.dynamic_index_in_dim(new_lat, request_pick, axis=0, keepdims=True)
    own_new_rope = lax.dynamic_index_in_dim(new_rope, request_pick, axis=0, keepdims=True)
    fresh_valid = lax.iota(jnp.int32, new_steps)[None, :] <= lax.iota(jnp.int32, new_steps)[:, None]
    fresh_valid = fresh_valid[None, :, :]
    fresh_part = block_partial(own_query, own_rope, own_lat, own_new_rope, fresh_valid)
    peak_val, weight_sum, summed = merge_pair(state, fresh_part)
    own_out = (summed / weight_sum[:, :, None]).astype(jnp.bfloat16)
    lat_out = butterfly_gather(own_out[0], "blk", range(low_bits))
    token_rows = requests * new_steps
    lat_head = lat_out.reshape(token_rows, latent_dim)
    heads_out = jnp.dot(lat_head, w_uv, preferred_element_type=jnp.float32).astype(jnp.bfloat16)
    proj_part = jnp.dot(heads_out, w_out, preferred_element_type=jnp.float32)
    projected = a2a_sum(proj_part, "blk")
    width = hidden_in.shape[2]
    mixed = hidden_in.reshape(token_rows, width).astype(jnp.float32) + projected
    meansq = jnp.mean(mixed * mixed, axis=1, keepdims=True)
    normed = (mixed * lax.rsqrt(meansq + NORM_EPS) * norm_gain[None, :]).astype(jnp.bfloat16)
    affinity = jax.nn.sigmoid(jnp.dot(normed, w_router, preferred_element_type=jnp.float32))
    expert_total = w_router.shape[1]
    top_count = routes.shape[2]
    flat_routes = routes.reshape(token_rows, top_count)
    route_hits = flat_routes[:, :, None] == lax.iota(jnp.int32, expert_total)[None, None, :]
    chosen = jnp.sum(jnp.where(route_hits, affinity[:, None, :], 0.0), axis=2)
    route_weight = ROUTE_SCALE * chosen / jnp.sum(chosen, axis=1, keepdims=True)
    local_count = w_gate.shape[0]
    local_ids = me * local_count + lax.iota(jnp.int32, local_count)
    pair_routes = flat_routes.reshape(token_rows * top_count)
    local_hits = (pair_routes[:, None] == local_ids[None, :]).astype(jnp.int32)
    ranks = jnp.cumsum(local_hits, axis=0) - 1
    slot_ids = lax.iota(jnp.int32, CAP)
    slot_match = local_hits.T[:, None, :] * (ranks.T[:, None, :] == slot_ids[None, :, None]).astype(
        jnp.int32
    )
    select = slot_match.reshape(local_count, CAP, token_rows, top_count).astype(jnp.float32)
    dispatch_map = jnp.sum(select, axis=3)
    combine_map = jnp.sum(select * route_weight[None, None, :, :], axis=3)
    dispatched = jnp.einsum(
        "esr,rd->esd", dispatch_map.astype(jnp.bfloat16), normed, preferred_element_type=jnp.float32
    ).astype(jnp.bfloat16)
    gathered = a2a_gather(dispatched, "exp")
    groups = gathered.shape[0]
    piece = gathered.transpose(1, 0, 2, 3).reshape(local_count, groups * CAP, width)
    gate = jnp.einsum("erd,edf->erf", piece, w_gate, preferred_element_type=jnp.float32)
    upper = jnp.einsum("erd,edf->erf", piece, w_up, preferred_element_type=jnp.float32)
    hidden_all = (jax.nn.silu(gate) * upper).astype(jnp.bfloat16)
    partial_out = jnp.einsum("erf,efd->erd", hidden_all, w_down, preferred_element_type=jnp.float32)
    groups_out = partial_out.reshape(local_count, groups, CAP, width).transpose(1, 0, 2, 3)
    expert_out = a2a_scatter_sum(groups_out, "exp")
    moe_part = jnp.einsum("esr,esd->rd", combine_map, expert_out, precision=lax.Precision.HIGHEST)
    count = lax.axis_size("blk")
    cols = width // count
    parts = moe_part.reshape(token_rows, count, cols).transpose(1, 0, 2).astype(jnp.bfloat16)
    moe_block = lax.all_to_all(parts, "blk", 0, 0, tiled=True).astype(jnp.float32).sum(axis=0)
    mixed_block = lax.dynamic_slice_in_dim(mixed, me * cols, cols, axis=1)
    result_block = (mixed_block + moe_block).astype(jnp.bfloat16)
    result = a2a_gather(result_block, "blk").transpose(1, 0, 2).reshape(token_rows, width)
    return result.reshape(requests, new_steps, width)


def solution(mesh):
    in_specs = (
        P("exp", None, None),
        P("exp", None, None, None),
        P("exp", None, None, None),
        P("exp", None, None),
        P("exp", None, None),
        P("exp", "blk", None),
        P("exp", "blk", None),
        P("exp"),
        P(None, "blk"),
        P("blk", None),
        P(),
        P(),
        P("exp", None, None),
        P("blk", None, "exp"),
        P("blk", None, "exp"),
        P("blk", "exp", None),
    )
    out_specs = P("exp", None, None)
    return jax.shard_map(local, mesh=mesh, in_specs=in_specs, out_specs=out_specs, check_vma=False)
```

```python
import jax
import jax.numpy as jnp
from jax import lax
from jax.sharding import PartitionSpec as P

V = 128
QK = 192
CAP = 3


NEG_FILL = -1e30
ROUTE_SCALE = 2.446
NORM_EPS = 1e-06


def xor_pairs(count, mask):
    return [(i, i ^ mask) for i in range(count)]


def exchange(x, axis, mask):
    count = lax.axis_size(axis)
    return jax.tree.map(lambda part: lax.ppermute(part, axis, xor_pairs(count, mask)), x)


def exchange_state(state, axis, mask):
    peak_val, weight_sum, summed = state
    packed = jnp.concatenate([summed, peak_val[..., None], weight_sum[..., None]], axis=-1)
    got = exchange(packed, axis, mask)
    width = summed.shape[-1]
    return (got[..., width], got[..., width + 1], got[..., :width])


def butterfly_sum(x, axis, bits):
    for bit in bits:
        x = x + exchange(x, axis, 1 << bit)
    return x


def butterfly_gather(x, axis, bits):
    me = lax.axis_index(axis)
    x = x[None]
    for bit in bits:
        other = exchange(x, axis, 1 << bit)
        high = ((me >> bit) & 1) == 1
        low_part = jnp.where(high, other, x)
        high_part = jnp.where(high, x, other)
        x = jnp.concatenate([low_part, high_part], axis=0)
    return x


def butterfly_scatter_sum(x, axis, bits):
    me = lax.axis_index(axis)
    for bit in bits:
        side = (me >> bit) & 1
        keep = lax.dynamic_index_in_dim(x, side, 0, keepdims=False)
        send = lax.dynamic_index_in_dim(x, 1 - side, 0, keepdims=False)
        x = keep + exchange(send, axis, 1 << bit)
    return x


def a2a_sum(x, axis):
    count = lax.axis_size(axis)
    rows, cols = x.shape
    parts = x.reshape(rows, count, cols // count).transpose(1, 0, 2).astype(jnp.bfloat16)
    mine = lax.all_to_all(parts, axis, 0, 0, tiled=True).astype(jnp.float32).sum(axis=0)
    spread = jnp.broadcast_to(mine[None], (count,) + mine.shape)
    back = lax.all_to_all(spread, axis, 0, 0, tiled=True)
    return back.transpose(1, 0, 2).reshape(rows, cols)


def a2a_gather(x, axis):
    count = lax.axis_size(axis)
    spread = jnp.broadcast_to(x[None], (count,) + x.shape)
    return lax.all_to_all(spread, axis, 0, 0, tiled=True)


def a2a_scatter_sum(x, axis):
    got = lax.all_to_all(x.astype(jnp.bfloat16), axis, 0, 0, tiled=True)
    return got.astype(jnp.float32).sum(axis=0)


def block_partial(query, query_rope, keys_lat, keys_rope, valid):
    scale = QK ** (-0.5)
    scores = (
        jnp.einsum("rmc,rkc->rmk", query, keys_lat, preferred_element_type=jnp.float32)
        + jnp.einsum("rmc,rkc->rmk", query_rope, keys_rope, preferred_element_type=jnp.float32)
    ) * scale
    masked = jnp.where(valid, scores, NEG_FILL)
    peak_val = jnp.max(masked, axis=2)
    weights = jnp.where(valid, jnp.exp(masked - peak_val[:, :, None]), 0.0)
    weight_sum = jnp.sum(weights, axis=2)
    summed = jnp.einsum(
        "rmk,rkc->rmc", weights.astype(jnp.bfloat16), keys_lat, preferred_element_type=jnp.float32
    )
    return (peak_val, weight_sum, summed)


def merge_pair(left_part, right_part):
    peak_left, total_left, sum_left = left_part
    peak_right, total_right, sum_right = right_part
    peak_val = jnp.maximum(peak_left, peak_right)
    factor_left = jnp.exp(peak_left - peak_val)
    factor_right = jnp.exp(peak_right - peak_val)
    weight_sum = factor_left * total_left + factor_right * total_right
    summed = factor_left[..., None] * sum_left + factor_right[..., None] * sum_right
    return (peak_val, weight_sum, summed)


def merge_packed(left, right, width):
    peak_val, weight_sum, summed = merge_pair(
        (left[..., width], left[..., width + 1], left[..., :width]),
        (right[..., width], right[..., width + 1], right[..., :width]),
    )
    return jnp.concatenate([summed, peak_val[..., None], weight_sum[..., None]], axis=-1)


def local(
    hidden_in,
    q_lat,
    q_rope,
    new_lat,
    new_rope,
    cache_lat,
    cache_rope,
    lengths,
    w_uv,
    w_out,
    norm_gain,
    w_router,
    routes,
    w_gate,
    w_up,
    w_down,
):
    requests, new_steps, head_count, latent_dim = q_lat.shape
    me = lax.axis_index("blk")
    blk_bits = lax.axis_size("blk").bit_length() - 1
    exp_bits = lax.axis_size("exp").bit_length() - 1
    query_rows = new_steps * head_count
    query = q_lat.reshape(requests, query_rows, latent_dim)
    query_rope = q_rope.reshape(requests, query_rows, q_rope.shape[3])
    cache_span = cache_lat.shape[1]
    position = me * cache_span + lax.iota(jnp.int32, cache_span)
    cache_valid = jnp.broadcast_to(
        position[None, None, :] < lengths[:, None, None], (requests, query_rows, cache_span)
    )
    peak_val, weight_sum, summed = block_partial(query, query_rope, cache_lat, cache_rope, cache_valid)
    head_bits = head_count.bit_length() - 1
    low_bits = blk_bits - head_bits
    packed = jnp.concatenate([summed, peak_val[..., None], weight_sum[..., None]], axis=-1)
    packed = packed.reshape((2,) * low_bits + (query_rows, latent_dim + 2))
    for bit in range(low_bits):
        axis_pos = low_bits - 1 - bit
        side = (me >> bit) & 1
        keep = lax.dynamic_index_in_dim(packed, side, axis_pos, keepdims=False)
        send = lax.dynamic_index_in_dim(packed, 1 - side, axis_pos, keepdims=False)
        packed = merge_packed(keep, exchange(send, "blk", 1 << bit), latent_dim)
    packed = packed.reshape(new_steps, head_count, latent_dim + 2).transpose(1, 0, 2)
    flat = packed.reshape(head_count, new_steps * (latent_dim + 2))
    quad = 1 << low_bits
    owners = [[slot + quad * h for h in range(head_count)] for slot in range(quad)]
    got = lax.all_to_all(flat, "blk", 0, 0, tiled=True, axis_index_groups=owners)
    got = got.reshape(head_count, new_steps, latent_dim + 2)
    peaks = got[..., latent_dim]
    totals = got[..., latent_dim + 1]
    peak_all = jnp.max(peaks, axis=0)
    factors = jnp.exp(peaks - peak_all[None])
    state = (
        peak_all[None],
        jnp.sum(factors * totals, axis=0)[None],
        jnp.sum(factors[..., None] * got[..., :latent_dim], axis=0)[None],
    )
    head_pick = me >> low_bits
    request_pick = me & ((1 << low_bits) - 1)
    own_query = lax.dynamic_index_in_dim(q_lat, request_pick, axis=0, keepdims=True)
    own_query = lax.dynamic_index_in_dim(own_query, head_pick, axis=2, keepdims=False)
    own_rope = lax.dynamic_index_in_dim(q_rope, request_pick, axis=0, keepdims=True)
    own_rope = lax.dynamic_index_in_dim(own_rope, head_pick, axis=2, keepdims=False)
    own_lat = lax.dynamic_index_in_dim(new_lat, request_pick, axis=0, keepdims=True)
    own_new_rope = lax.dynamic_index_in_dim(new_rope, request_pick, axis=0, keepdims=True)
    fresh_valid = lax.iota(jnp.int32, new_steps)[None, :] <= lax.iota(jnp.int32, new_steps)[:, None]
    fresh_valid = fresh_valid[None, :, :]
    fresh_part = block_partial(own_query, own_rope, own_lat, own_new_rope, fresh_valid)
    peak_val, weight_sum, summed = merge_pair(state, fresh_part)
    own_out = (summed / weight_sum[:, :, None]).astype(jnp.bfloat16)
    lat_out = butterfly_gather(own_out[0], "blk", range(low_bits))
    token_rows = requests * new_steps
    lat_head = lat_out.reshape(token_rows, latent_dim)
    heads_out = jnp.dot(lat_head, w_uv, preferred_element_type=jnp.float32).astype(jnp.bfloat16)
    proj_part = jnp.dot(heads_out, w_out, preferred_element_type=jnp.float32)
    projected = a2a_sum(proj_part, "blk")
    width = hidden_in.shape[2]
    mixed = hidden_in.reshape(token_rows, width).astype(jnp.float32) + projected
    meansq = jnp.mean(mixed * mixed, axis=1, keepdims=True)
    normed = (mixed * lax.rsqrt(meansq + NORM_EPS) * norm_gain[None, :]).astype(jnp.bfloat16)
    affinity = jax.nn.sigmoid(jnp.dot(normed, w_router, preferred_element_type=jnp.float32))
    expert_total = w_router.shape[1]
    top_count = routes.shape[2]
    flat_routes = routes.reshape(token_rows, top_count)
    route_hits = flat_routes[:, :, None] == lax.iota(jnp.int32, expert_total)[None, None, :]
    chosen = jnp.sum(jnp.where(route_hits, affinity[:, None, :], 0.0), axis=2)
    route_weight = ROUTE_SCALE * chosen / jnp.sum(chosen, axis=1, keepdims=True)
    local_count = w_gate.shape[0]
    local_ids = me * local_count + lax.iota(jnp.int32, local_count)
    pair_routes = flat_routes.reshape(token_rows * top_count)
    local_hits = (pair_routes[:, None] == local_ids[None, :]).astype(jnp.int32)
    ranks = jnp.cumsum(local_hits, axis=0) - 1
    slot_ids = lax.iota(jnp.int32, CAP)
    slot_match = local_hits.T[:, None, :] * (ranks.T[:, None, :] == slot_ids[None, :, None]).astype(
        jnp.int32
    )
    select = slot_match.reshape(local_count, CAP, token_rows, top_count).astype(jnp.float32)
    dispatch_map = jnp.sum(select, axis=3)
    combine_map = jnp.sum(select * route_weight[None, None, :, :], axis=3)
    dispatched = jnp.einsum(
        "esr,rd->esd", dispatch_map.astype(jnp.bfloat16), normed, preferred_element_type=jnp.float32
    ).astype(jnp.bfloat16)
    gathered = a2a_gather(dispatched, "exp")
    groups = gathered.shape[0]
    piece = gathered.transpose(1, 0, 2, 3).reshape(local_count, groups * CAP, width)
    gate = jnp.einsum("erd,edf->erf", piece, w_gate, preferred_element_type=jnp.float32)
    upper = jnp.einsum("erd,edf->erf", piece, w_up, preferred_element_type=jnp.float32)
    hidden_all = (jax.nn.silu(gate) * upper).astype(jnp.bfloat16)
    partial_out = jnp.einsum("erf,efd->erd", hidden_all, w_down, preferred_element_type=jnp.float32)
    groups_out = partial_out.reshape(local_count, groups, CAP, width).transpose(1, 0, 2, 3)
    expert_out = a2a_scatter_sum(groups_out, "exp")
    moe_part = jnp.einsum("esr,esd->rd", combine_map, expert_out, precision=lax.Precision.HIGHEST)
    count = lax.axis_size("blk")
    cols = width // count
    parts = moe_part.reshape(token_rows, count, cols).transpose(1, 0, 2).astype(jnp.bfloat16)
    moe_block = lax.all_to_all(parts, "blk", 0, 0, tiled=True).astype(jnp.float32).sum(axis=0)
    mixed_block = lax.dynamic_slice_in_dim(mixed, me * cols, cols, axis=1)
    result_block = (mixed_block + moe_block).astype(jnp.bfloat16)
    result = a2a_gather(result_block, "blk").transpose(1, 0, 2).reshape(token_rows, width)
    return result.reshape(requests, new_steps, width)


def solution(mesh):
    in_specs = (
        P("exp", None, None),
        P("exp", None, None, None),
        P("exp", None, None, None),
        P("exp", None, None),
        P("exp", None, None),
        P("exp", "blk", None),
        P("exp", "blk", None),
        P("exp"),
        P(None, "blk"),
        P("blk", None),
        P(),
        P(),
        P("exp", None, None),
        P("blk", None, "exp"),
        P("blk", None, "exp"),
        P("blk", "exp", None),
    )
    out_specs = P("exp", None, None)
    return jax.shard_map(local, mesh=mesh, in_specs=in_specs, out_specs=out_specs, check_vma=False)
```

```python
import jax
import jax.numpy as jnp
from jax import lax
from jax.sharding import PartitionSpec as P

V = 128
QK = 192
CAP = 3


NEG_FILL = -1e30
ROUTE_SCALE = 2.446
NORM_EPS = 1e-06


def xor_pairs(count, mask):
    return [(i, i ^ mask) for i in range(count)]


def exchange(x, axis, mask):
    count = lax.axis_size(axis)
    return jax.tree.map(lambda part: lax.ppermute(part, axis, xor_pairs(count, mask)), x)


def exchange_state(state, axis, mask):
    peak_val, weight_sum, summed = state
    packed = jnp.concatenate([summed, peak_val[..., None], weight_sum[..., None]], axis=-1)
    got = exchange(packed, axis, mask)
    width = summed.shape[-1]
    return (got[..., width], got[..., width + 1], got[..., :width])


def butterfly_sum(x, axis, bits):
    for bit in bits:
        x = x + exchange(x, axis, 1 << bit)
    return x


def butterfly_gather(x, axis, bits):
    me = lax.axis_index(axis)
    x = x[None]
    for bit in bits:
        other = exchange(x, axis, 1 << bit)
        high = ((me >> bit) & 1) == 1
        low_part = jnp.where(high, other, x)
        high_part = jnp.where(high, x, other)
        x = jnp.concatenate([low_part, high_part], axis=0)
    return x


def butterfly_scatter_sum(x, axis, bits):
    me = lax.axis_index(axis)
    for bit in bits:
        side = (me >> bit) & 1
        keep = lax.dynamic_index_in_dim(x, side, 0, keepdims=False)
        send = lax.dynamic_index_in_dim(x, 1 - side, 0, keepdims=False)
        x = keep + exchange(send, axis, 1 << bit)
    return x


def a2a_sum(x, axis):
    count = lax.axis_size(axis)
    rows, cols = x.shape
    parts = x.reshape(rows, count, cols // count).transpose(1, 0, 2).astype(jnp.bfloat16)
    mine = lax.all_to_all(parts, axis, 0, 0, tiled=True).astype(jnp.float32).sum(axis=0)
    spread = jnp.broadcast_to(mine.astype(jnp.bfloat16)[None], (count,) + mine.shape)
    back = lax.all_to_all(spread, axis, 0, 0, tiled=True).astype(jnp.float32)
    return back.transpose(1, 0, 2).reshape(rows, cols)


def a2a_gather(x, axis):
    count = lax.axis_size(axis)
    spread = jnp.broadcast_to(x[None], (count,) + x.shape)
    return lax.all_to_all(spread, axis, 0, 0, tiled=True)


def a2a_scatter_sum(x, axis):
    got = lax.all_to_all(x.astype(jnp.bfloat16), axis, 0, 0, tiled=True)
    return got.astype(jnp.float32).sum(axis=0)


def block_partial(query, query_rope, keys_lat, keys_rope, valid):
    scale = QK ** (-0.5)
    scores = (
        jnp.einsum("rmc,rkc->rmk", query, keys_lat, preferred_element_type=jnp.float32)
        + jnp.einsum("rmc,rkc->rmk", query_rope, keys_rope, preferred_element_type=jnp.float32)
    ) * scale
    masked = jnp.where(valid, scores, NEG_FILL)
    peak_val = jnp.max(masked, axis=2)
    weights = jnp.where(valid, jnp.exp(masked - peak_val[:, :, None]), 0.0)
    weight_sum = jnp.sum(weights, axis=2)
    summed = jnp.einsum(
        "rmk,rkc->rmc", weights.astype(jnp.bfloat16), keys_lat, preferred_element_type=jnp.float32
    )
    return (peak_val, weight_sum, summed)


def merge_pair(left_part, right_part):
    peak_left, total_left, sum_left = left_part
    peak_right, total_right, sum_right = right_part
    peak_val = jnp.maximum(peak_left, peak_right)
    factor_left = jnp.exp(peak_left - peak_val)
    factor_right = jnp.exp(peak_right - peak_val)
    weight_sum = factor_left * total_left + factor_right * total_right
    summed = factor_left[..., None] * sum_left + factor_right[..., None] * sum_right
    return (peak_val, weight_sum, summed)


def merge_packed(left, right, width):
    peak_val, weight_sum, summed = merge_pair(
        (left[..., width], left[..., width + 1], left[..., :width]),
        (right[..., width], right[..., width + 1], right[..., :width]),
    )
    return jnp.concatenate([summed, peak_val[..., None], weight_sum[..., None]], axis=-1)


def local(
    hidden_in,
    q_lat,
    q_rope,
    new_lat,
    new_rope,
    cache_lat,
    cache_rope,
    lengths,
    w_uv,
    w_out,
    norm_gain,
    w_router,
    routes,
    w_gate,
    w_up,
    w_down,
):
    requests, new_steps, head_count, latent_dim = q_lat.shape
    me = lax.axis_index("blk")
    blk_bits = lax.axis_size("blk").bit_length() - 1
    exp_bits = lax.axis_size("exp").bit_length() - 1
    query_rows = new_steps * head_count
    query = q_lat.reshape(requests, query_rows, latent_dim)
    query_rope = q_rope.reshape(requests, query_rows, q_rope.shape[3])
    cache_span = cache_lat.shape[1]
    position = me * cache_span + lax.iota(jnp.int32, cache_span)
    cache_valid = jnp.broadcast_to(
        position[None, None, :] < lengths[:, None, None], (requests, query_rows, cache_span)
    )
    peak_val, weight_sum, summed = block_partial(query, query_rope, cache_lat, cache_rope, cache_valid)
    head_bits = head_count.bit_length() - 1
    low_bits = blk_bits - head_bits
    packed = jnp.concatenate([summed, peak_val[..., None], weight_sum[..., None]], axis=-1)
    packed = packed.reshape((2,) * low_bits + (query_rows, latent_dim + 2))
    for bit in range(low_bits):
        axis_pos = low_bits - 1 - bit
        side = (me >> bit) & 1
        keep = lax.dynamic_index_in_dim(packed, side, axis_pos, keepdims=False)
        send = lax.dynamic_index_in_dim(packed, 1 - side, axis_pos, keepdims=False)
        packed = merge_packed(keep, exchange(send, "blk", 1 << bit), latent_dim)
    packed = packed.reshape(new_steps, head_count, latent_dim + 2).transpose(1, 0, 2)
    flat = packed.reshape(head_count, new_steps * (latent_dim + 2))
    quad = 1 << low_bits
    owners = [[slot + quad * h for h in range(head_count)] for slot in range(quad)]
    got = lax.all_to_all(flat, "blk", 0, 0, tiled=True, axis_index_groups=owners)
    got = got.reshape(head_count, new_steps, latent_dim + 2)
    peaks = got[..., latent_dim]
    totals = got[..., latent_dim + 1]
    peak_all = jnp.max(peaks, axis=0)
    factors = jnp.exp(peaks - peak_all[None])
    state = (
        peak_all[None],
        jnp.sum(factors * totals, axis=0)[None],
        jnp.sum(factors[..., None] * got[..., :latent_dim], axis=0)[None],
    )
    head_pick = me >> low_bits
    request_pick = me & ((1 << low_bits) - 1)
    own_query = lax.dynamic_index_in_dim(q_lat, request_pick, axis=0, keepdims=True)
    own_query = lax.dynamic_index_in_dim(own_query, head_pick, axis=2, keepdims=False)
    own_rope = lax.dynamic_index_in_dim(q_rope, request_pick, axis=0, keepdims=True)
    own_rope = lax.dynamic_index_in_dim(own_rope, head_pick, axis=2, keepdims=False)
    own_lat = lax.dynamic_index_in_dim(new_lat, request_pick, axis=0, keepdims=True)
    own_new_rope = lax.dynamic_index_in_dim(new_rope, request_pick, axis=0, keepdims=True)
    fresh_valid = lax.iota(jnp.int32, new_steps)[None, :] <= lax.iota(jnp.int32, new_steps)[:, None]
    fresh_valid = fresh_valid[None, :, :]
    fresh_part = block_partial(own_query, own_rope, own_lat, own_new_rope, fresh_valid)
    peak_val, weight_sum, summed = merge_pair(state, fresh_part)
    own_out = (summed / weight_sum[:, :, None]).astype(jnp.bfloat16)
    lat_out = butterfly_gather(own_out[0], "blk", range(low_bits))
    token_rows = requests * new_steps
    lat_head = lat_out.reshape(token_rows, latent_dim)
    heads_out = jnp.dot(lat_head, w_uv, preferred_element_type=jnp.float32).astype(jnp.bfloat16)
    proj_part = jnp.dot(heads_out, w_out, preferred_element_type=jnp.float32)
    projected = a2a_sum(proj_part, "blk")
    width = hidden_in.shape[2]
    mixed = hidden_in.reshape(token_rows, width).astype(jnp.float32) + projected
    meansq = jnp.mean(mixed * mixed, axis=1, keepdims=True)
    normed = (mixed * lax.rsqrt(meansq + NORM_EPS) * norm_gain[None, :]).astype(jnp.bfloat16)
    affinity = jax.nn.sigmoid(jnp.dot(normed, w_router, preferred_element_type=jnp.float32))
    expert_total = w_router.shape[1]
    top_count = routes.shape[2]
    flat_routes = routes.reshape(token_rows, top_count)
    route_hits = flat_routes[:, :, None] == lax.iota(jnp.int32, expert_total)[None, None, :]
    chosen = jnp.sum(jnp.where(route_hits, affinity[:, None, :], 0.0), axis=2)
    route_weight = ROUTE_SCALE * chosen / jnp.sum(chosen, axis=1, keepdims=True)
    local_count = w_gate.shape[0]
    local_ids = me * local_count + lax.iota(jnp.int32, local_count)
    pair_routes = flat_routes.reshape(token_rows * top_count)
    local_hits = (pair_routes[:, None] == local_ids[None, :]).astype(jnp.int32)
    ranks = jnp.cumsum(local_hits, axis=0) - 1
    slot_ids = lax.iota(jnp.int32, CAP)
    slot_match = local_hits.T[:, None, :] * (ranks.T[:, None, :] == slot_ids[None, :, None]).astype(
        jnp.int32
    )
    select = slot_match.reshape(local_count, CAP, token_rows, top_count).astype(jnp.float32)
    dispatch_map = jnp.sum(select, axis=3)
    combine_map = jnp.sum(select * route_weight[None, None, :, :], axis=3)
    dispatched = jnp.einsum(
        "esr,rd->esd", dispatch_map.astype(jnp.bfloat16), normed, preferred_element_type=jnp.float32
    ).astype(jnp.bfloat16)
    gathered = a2a_gather(dispatched, "exp")
    groups = gathered.shape[0]
    piece = gathered.transpose(1, 0, 2, 3).reshape(local_count, groups * CAP, width)
    gate = jnp.einsum("erd,edf->erf", piece, w_gate, preferred_element_type=jnp.float32)
    upper = jnp.einsum("erd,edf->erf", piece, w_up, preferred_element_type=jnp.float32)
    hidden_all = (jax.nn.silu(gate) * upper).astype(jnp.bfloat16)
    partial_out = jnp.einsum("erf,efd->erd", hidden_all, w_down, preferred_element_type=jnp.float32)
    groups_out = partial_out.reshape(local_count, groups, CAP, width).transpose(1, 0, 2, 3)
    expert_out = a2a_scatter_sum(groups_out, "exp")
    moe_part = jnp.einsum("esr,esd->rd", combine_map, expert_out, precision=lax.Precision.HIGHEST)
    count = lax.axis_size("blk")
    cols = width // count
    parts = moe_part.reshape(token_rows, count, cols).transpose(1, 0, 2).astype(jnp.bfloat16)
    moe_block = lax.all_to_all(parts, "blk", 0, 0, tiled=True).astype(jnp.float32).sum(axis=0)
    mixed_block = lax.dynamic_slice_in_dim(mixed, me * cols, cols, axis=1)
    result_block = (mixed_block + moe_block).astype(jnp.bfloat16)
    result = a2a_gather(result_block, "blk").transpose(1, 0, 2).reshape(token_rows, width)
    return result.reshape(requests, new_steps, width)


def solution(mesh):
    in_specs = (
        P("exp", None, None),
        P("exp", None, None, None),
        P("exp", None, None, None),
        P("exp", None, None),
        P("exp", None, None),
        P("exp", "blk", None),
        P("exp", "blk", None),
        P("exp"),
        P(None, "blk"),
        P("blk", None),
        P(),
        P(),
        P("exp", None, None),
        P("blk", None, "exp"),
        P("blk", None, "exp"),
        P("blk", "exp", None),
    )
    out_specs = P("exp", None, None)
    return jax.shard_map(local, mesh=mesh, in_specs=in_specs, out_specs=out_specs, check_vma=False)
```

```python
import jax
import jax.numpy as jnp
from jax import lax
from jax.sharding import PartitionSpec as P

V = 128
QK = 192
CAP = 3


NEG_FILL = -1e30
ROUTE_SCALE = 2.446
NORM_EPS = 1e-06


def xor_pairs(count, mask):
    return [(i, i ^ mask) for i in range(count)]


def exchange(x, axis, mask):
    count = lax.axis_size(axis)
    return jax.tree.map(lambda part: lax.ppermute(part, axis, xor_pairs(count, mask)), x)


def exchange_state(state, axis, mask):
    peak_val, weight_sum, summed = state
    packed = jnp.concatenate([summed, peak_val[..., None], weight_sum[..., None]], axis=-1)
    got = exchange(packed, axis, mask)
    width = summed.shape[-1]
    return (got[..., width], got[..., width + 1], got[..., :width])


def butterfly_sum(x, axis, bits):
    for bit in bits:
        x = x + exchange(x, axis, 1 << bit)
    return x


def butterfly_gather(x, axis, bits):
    me = lax.axis_index(axis)
    x = x[None]
    for bit in bits:
        other = exchange(x, axis, 1 << bit)
        high = ((me >> bit) & 1) == 1
        low_part = jnp.where(high, other, x)
        high_part = jnp.where(high, x, other)
        x = jnp.concatenate([low_part, high_part], axis=0)
    return x


def butterfly_scatter_sum(x, axis, bits):
    me = lax.axis_index(axis)
    for bit in bits:
        side = (me >> bit) & 1
        keep = lax.dynamic_index_in_dim(x, side, 0, keepdims=False)
        send = lax.dynamic_index_in_dim(x, 1 - side, 0, keepdims=False)
        x = keep + exchange(send, axis, 1 << bit)
    return x


def a2a_sum(x, axis):
    count = lax.axis_size(axis)
    rows, cols = x.shape
    parts = x.reshape(rows, count, cols // count).transpose(1, 0, 2).astype(jnp.bfloat16)
    mine = lax.all_to_all(parts, axis, 0, 0, tiled=True).astype(jnp.float32).sum(axis=0)
    spread = jnp.broadcast_to(mine.astype(jnp.bfloat16)[None], (count,) + mine.shape)
    back = lax.all_to_all(spread, axis, 0, 0, tiled=True).astype(jnp.float32)
    return back.transpose(1, 0, 2).reshape(rows, cols)


def a2a_gather(x, axis):
    count = lax.axis_size(axis)
    spread = jnp.broadcast_to(x[None], (count,) + x.shape)
    return lax.all_to_all(spread, axis, 0, 0, tiled=True)


def a2a_scatter_sum(x, axis):
    got = lax.all_to_all(x.astype(jnp.bfloat16), axis, 0, 0, tiled=True)
    return got.astype(jnp.float32).sum(axis=0)


def block_partial(query, query_rope, keys_lat, keys_rope, valid):
    scale = QK ** (-0.5)
    scores = (
        jnp.einsum("rmc,rkc->rmk", query, keys_lat, preferred_element_type=jnp.float32)
        + jnp.einsum("rmc,rkc->rmk", query_rope, keys_rope, preferred_element_type=jnp.float32)
    ) * scale
    masked = jnp.where(valid, scores, NEG_FILL)
    peak_val = jnp.max(masked, axis=2)
    weights = jnp.where(valid, jnp.exp(masked - peak_val[:, :, None]), 0.0)
    weight_sum = jnp.sum(weights, axis=2)
    summed = jnp.einsum(
        "rmk,rkc->rmc", weights.astype(jnp.bfloat16), keys_lat, preferred_element_type=jnp.float32
    )
    return (peak_val, weight_sum, summed)


def merge_pair(left_part, right_part):
    peak_left, total_left, sum_left = left_part
    peak_right, total_right, sum_right = right_part
    peak_val = jnp.maximum(peak_left, peak_right)
    factor_left = jnp.exp(peak_left - peak_val)
    factor_right = jnp.exp(peak_right - peak_val)
    weight_sum = factor_left * total_left + factor_right * total_right
    summed = factor_left[..., None] * sum_left + factor_right[..., None] * sum_right
    return (peak_val, weight_sum, summed)


def merge_packed(left, right, width):
    peak_val, weight_sum, summed = merge_pair(
        (left[..., width], left[..., width + 1], left[..., :width]),
        (right[..., width], right[..., width + 1], right[..., :width]),
    )
    return jnp.concatenate([summed, peak_val[..., None], weight_sum[..., None]], axis=-1)


def local(
    hidden_in,
    q_lat,
    q_rope,
    new_lat,
    new_rope,
    cache_lat,
    cache_rope,
    lengths,
    w_uv,
    w_out,
    norm_gain,
    w_router,
    routes,
    w_gate,
    w_up,
    w_down,
):
    requests, new_steps, head_count, latent_dim = q_lat.shape
    me = lax.axis_index("blk")
    blk_bits = lax.axis_size("blk").bit_length() - 1
    exp_bits = lax.axis_size("exp").bit_length() - 1
    query_rows = new_steps * head_count
    query = q_lat.reshape(requests, query_rows, latent_dim)
    query_rope = q_rope.reshape(requests, query_rows, q_rope.shape[3])
    cache_span = cache_lat.shape[1]
    position = me * cache_span + lax.iota(jnp.int32, cache_span)
    cache_valid = jnp.broadcast_to(
        position[None, None, :] < lengths[:, None, None], (requests, query_rows, cache_span)
    )
    peak_val, weight_sum, summed = block_partial(query, query_rope, cache_lat, cache_rope, cache_valid)
    head_bits = head_count.bit_length() - 1
    low_bits = blk_bits - head_bits
    packed = jnp.concatenate([summed, peak_val[..., None], weight_sum[..., None]], axis=-1)
    packed = packed.reshape((2,) * low_bits + (query_rows, latent_dim + 2))
    for bit in range(low_bits):
        axis_pos = low_bits - 1 - bit
        side = (me >> bit) & 1
        keep = lax.dynamic_index_in_dim(packed, side, axis_pos, keepdims=False)
        send = lax.dynamic_index_in_dim(packed, 1 - side, axis_pos, keepdims=False)
        packed = merge_packed(keep, exchange(send, "blk", 1 << bit), latent_dim)
    packed = packed.reshape(new_steps, head_count, latent_dim + 2).transpose(1, 0, 2)
    top = blk_bits - 1
    half = head_count // 2
    packed = packed.reshape(2, half, new_steps, latent_dim + 2)
    side = (me >> top) & 1
    keep = lax.dynamic_index_in_dim(packed, side, 0, keepdims=False)
    send = lax.dynamic_index_in_dim(packed, 1 - side, 0, keepdims=False)
    packed = merge_packed(keep, exchange(send, "blk", 1 << top), latent_dim)
    flat = packed.reshape(half, new_steps * (latent_dim + 2))
    quad = 1 << low_bits
    owners = [[slot + quad * (upper * half + h) for h in range(half)] for upper in range(2) for slot in range(quad)]
    got = lax.all_to_all(flat, "blk", 0, 0, tiled=True, axis_index_groups=owners)
    got = got.reshape(half, new_steps, latent_dim + 2)
    peaks = got[..., latent_dim]
    totals = got[..., latent_dim + 1]
    peak_all = jnp.max(peaks, axis=0)
    factors = jnp.exp(peaks - peak_all[None])
    state = (
        peak_all[None],
        jnp.sum(factors * totals, axis=0)[None],
        jnp.sum(factors[..., None] * got[..., :latent_dim], axis=0)[None],
    )
    head_pick = me >> low_bits
    request_pick = me & ((1 << low_bits) - 1)
    own_query = lax.dynamic_index_in_dim(q_lat, request_pick, axis=0, keepdims=True)
    own_query = lax.dynamic_index_in_dim(own_query, head_pick, axis=2, keepdims=False)
    own_rope = lax.dynamic_index_in_dim(q_rope, request_pick, axis=0, keepdims=True)
    own_rope = lax.dynamic_index_in_dim(own_rope, head_pick, axis=2, keepdims=False)
    own_lat = lax.dynamic_index_in_dim(new_lat, request_pick, axis=0, keepdims=True)
    own_new_rope = lax.dynamic_index_in_dim(new_rope, request_pick, axis=0, keepdims=True)
    fresh_valid = lax.iota(jnp.int32, new_steps)[None, :] <= lax.iota(jnp.int32, new_steps)[:, None]
    fresh_valid = fresh_valid[None, :, :]
    fresh_part = block_partial(own_query, own_rope, own_lat, own_new_rope, fresh_valid)
    peak_val, weight_sum, summed = merge_pair(state, fresh_part)
    own_out = (summed / weight_sum[:, :, None]).astype(jnp.bfloat16)
    lat_out = butterfly_gather(own_out[0], "blk", range(low_bits))
    token_rows = requests * new_steps
    lat_head = lat_out.reshape(token_rows, latent_dim)
    heads_out = jnp.dot(lat_head, w_uv, preferred_element_type=jnp.float32).astype(jnp.bfloat16)
    proj_part = jnp.dot(heads_out, w_out, preferred_element_type=jnp.float32)
    projected = a2a_sum(proj_part, "blk")
    width = hidden_in.shape[2]
    mixed = hidden_in.reshape(token_rows, width).astype(jnp.float32) + projected
    meansq = jnp.mean(mixed * mixed, axis=1, keepdims=True)
    normed = (mixed * lax.rsqrt(meansq + NORM_EPS) * norm_gain[None, :]).astype(jnp.bfloat16)
    affinity = jax.nn.sigmoid(jnp.dot(normed, w_router, preferred_element_type=jnp.float32))
    expert_total = w_router.shape[1]
    top_count = routes.shape[2]
    flat_routes = routes.reshape(token_rows, top_count)
    route_hits = flat_routes[:, :, None] == lax.iota(jnp.int32, expert_total)[None, None, :]
    chosen = jnp.sum(jnp.where(route_hits, affinity[:, None, :], 0.0), axis=2)
    route_weight = ROUTE_SCALE * chosen / jnp.sum(chosen, axis=1, keepdims=True)
    local_count = w_gate.shape[0]
    local_ids = me * local_count + lax.iota(jnp.int32, local_count)
    pair_routes = flat_routes.reshape(token_rows * top_count)
    local_hits = (pair_routes[:, None] == local_ids[None, :]).astype(jnp.int32)
    ranks = jnp.cumsum(local_hits, axis=0) - 1
    slot_ids = lax.iota(jnp.int32, CAP)
    slot_match = local_hits.T[:, None, :] * (ranks.T[:, None, :] == slot_ids[None, :, None]).astype(
        jnp.int32
    )
    select = slot_match.reshape(local_count, CAP, token_rows, top_count).astype(jnp.float32)
    dispatch_map = jnp.sum(select, axis=3)
    combine_map = jnp.sum(select * route_weight[None, None, :, :], axis=3)
    dispatched = jnp.einsum(
        "esr,rd->esd", dispatch_map.astype(jnp.bfloat16), normed, preferred_element_type=jnp.float32
    ).astype(jnp.bfloat16)
    gathered = a2a_gather(dispatched, "exp")
    groups = gathered.shape[0]
    piece = gathered.transpose(1, 0, 2, 3).reshape(local_count, groups * CAP, width)
    gate = jnp.einsum("erd,edf->erf", piece, w_gate, preferred_element_type=jnp.float32)
    upper = jnp.einsum("erd,edf->erf", piece, w_up, preferred_element_type=jnp.float32)
    hidden_all = (jax.nn.silu(gate) * upper).astype(jnp.bfloat16)
    partial_out = jnp.einsum("erf,efd->erd", hidden_all, w_down, preferred_element_type=jnp.float32)
    groups_out = partial_out.reshape(local_count, groups, CAP, width).transpose(1, 0, 2, 3)
    expert_out = a2a_scatter_sum(groups_out, "exp")
    moe_part = jnp.einsum("esr,esd->rd", combine_map, expert_out, precision=lax.Precision.HIGHEST)
    count = lax.axis_size("blk")
    cols = width // count
    parts = moe_part.reshape(token_rows, count, cols).transpose(1, 0, 2).astype(jnp.bfloat16)
    moe_block = lax.all_to_all(parts, "blk", 0, 0, tiled=True).astype(jnp.float32).sum(axis=0)
    mixed_block = lax.dynamic_slice_in_dim(mixed, me * cols, cols, axis=1)
    result_block = (mixed_block + moe_block).astype(jnp.bfloat16)
    result = a2a_gather(result_block, "blk").transpose(1, 0, 2).reshape(token_rows, width)
    return result.reshape(requests, new_steps, width)


def solution(mesh):
    in_specs = (
        P("exp", None, None),
        P("exp", None, None, None),
        P("exp", None, None, None),
        P("exp", None, None),
        P("exp", None, None),
        P("exp", "blk", None),
        P("exp", "blk", None),
        P("exp"),
        P(None, "blk"),
        P("blk", None),
        P(),
        P(),
        P("exp", None, None),
        P("blk", None, "exp"),
        P("blk", None, "exp"),
        P("blk", "exp", None),
    )
    out_specs = P("exp", None, None)
    return jax.shard_map(local, mesh=mesh, in_specs=in_specs, out_specs=out_specs, check_vma=False)
```
